32 devices in a mesh: groups: 2 (over x), ctx: 8 (over z, y), dp: 2 (over core).
Axes of the slice: x: 2, y: 2, z: 4, core: 2. Of those that a mesh axis runs over, the one named last changes fastest.
Arguments:
- query_rows: bfloat16 [4, 3072, 4096], P(('groups', 'dp'), 'ctx'), parts along dimension 0, may hold values from -6 to 6
- key_rows: bfloat16 [4, 3072, 4096], P(('groups', 'dp'), 'ctx'), parts along dimension 0, may hold values from -6 to 6
- value_rows: bfloat16 [4, 3072, 4096], P(('groups', 'dp'), 'ctx'), parts along dimension 0, may hold values from -6 to 6
- gain: float32 [4096], P('dp'), may hold values from 0.5 to 1.5
Outputs:
- normed: bfloat16 [4, 3072, 4096], P(('groups', 'dp'), 'ctx'), parts along dimension 0
The draws below stay inside these ranges and needn't reach their ends.
There are 2 independent parts, one for each index of `groups`. The reference program is written for one: setup_inputs(seed, part) draws one part's arguments, and reference() takes and returns one part's arrays. A program takes and returns all parts, laid end to end along the dimension named above; an argument that names none is the same for every part. Nothing has to cross between parts.
All inputs are finite; a program needn't handle non-finite values.
Results may differ from the reference program's by a relative error of at most 0.0049.
Values may be sent and summed in bfloat16 or wider, within the bound.
No kernel may reach another device: no remote copies, remote signals or barrier semaphores. Data moves between devices by JAX's collectives and lax.ppermute only.
A program may use at most 192 MiB of HBM per device.

```python
import jax
import jax.numpy as jnp
from jax import lax

H = 32
DH = 128
T_DEV = 384
TOKENS = 3072
SEQS = 2


def levels(key, extent, pieces, smallest, largest):
    def one(dim, blocks):
        draws = jax.random.uniform(jax.random.fold_in(jax.random.fold_in(key, 6), dim), (blocks,), jnp.float32, smallest / len(pieces), largest / len(pieces))
        return jnp.repeat(jnp.exp(draws), extent[dim] // blocks).reshape((-1,) + (1,) * (len(extent) - dim - 1))

    level = one(*pieces[0])
    for cut in pieces[1:]:
        level = level * one(*cut)
    return level


def normal_values(own_key, dims, width, most, pieces=(), kind=jnp.bfloat16):
    values = jax.random.normal(own_key, dims, jnp.float32) * width
    if len(pieces) > 0:
        values = levels(own_key, dims, pieces, -0.22, 0.18) * values
    return jnp.clip(values, min=-most, max=most).astype(kind)


def setup_inputs(seed: int = 0, part: int = 0) -> dict:
    arg_keys = jax.random.split(jax.random.key(seed), 5)
    part_splits = jax.random.split(jax.random.fold_in(arg_keys[4], part), 5)
    return {
        "query_rows": normal_values(part_splits[0], (SEQS, TOKENS, H * DH), 1.0, 6.0, ((0, 2), (1, 8))),
        "key_rows": normal_values(part_splits[1], (SEQS, TOKENS, H * DH), 1.0, 6.0, ((0, 2), (1, 8))),
        "value_rows": normal_values(part_splits[2], (SEQS, TOKENS, H * DH), 1.0, 6.0, ((0, 2), (1, 8))),
        "gain": jnp.clip(1.0 + 0.1 * jax.random.normal(arg_keys[3], (H * DH,), jnp.float32), 0.5, 1.5),
    }


def reference(query_rows, key_rows, value_rows, gain):
    seq_count = query_rows.shape[0]
    block_count = query_rows.shape[1] // T_DEV

    def split(array):
        return array.reshape(seq_count, block_count, T_DEV, H, DH).transpose(1, 0, 2, 3, 4)
    causal_mask = jnp.arange(T_DEV)[:, None] >= jnp.arange(T_DEV)[None, :]

    def advance(state, block):
        query, keyset, valset = block
        query32 = query.astype(jnp.float32)
        key32 = keyset.astype(jnp.float32)
        val32 = valset.astype(jnp.float32)
        scores = jnp.einsum('sthd,suhd->shtu', query32, key32)
        masked = jnp.where(causal_mask, scores, 0.0).astype(jnp.bfloat16)
        weights = lax.optimization_barrier(masked).astype(jnp.float32)
        state_bf = lax.optimization_barrier(state.astype(jnp.bfloat16)).astype(jnp.float32)
        attended = jnp.einsum('shtu,suhe->sthe', weights, val32) + jnp.einsum('sthd,shde->sthe', query32, state_bf)
        new_state = state + jnp.einsum('sthd,sthe->shde', key32, val32)
        return (new_state, attended)
    start = jnp.zeros((seq_count, H, DH, DH), jnp.float32)
    _, outputs = lax.scan(advance, start, (split(query_rows), split(key_rows), split(value_rows)))
    attended = outputs.transpose(1, 0, 2, 3, 4).reshape(seq_count, block_count * T_DEV, H * DH)
    scale = lax.rsqrt(lax.optimization_barrier(jnp.mean(attended * attended, axis=-1, keepdims=True)) + 1e-05)
    return (attended * scale * gain).astype(jnp.bfloat16)
```

```python
import jax
import jax.numpy as jnp
from jax import lax
from jax.sharding import PartitionSpec as P

H = 32


def pair_chain_prefix(terms, axis):
    count = lax.axis_size(axis)
    mine_at = lax.axis_index(axis) % 2
    half = terms.shape[0] // 2
    pairs = count // 2
    mine = lax.dynamic_slice_in_dim(terms, mine_at * half, half, 0)
    other = lax.dynamic_slice_in_dim(terms, (1 - mine_at) * half, half, 0)
    swap = [(2 * i, 2 * i + 1) for i in range(pairs)] + [(2 * i + 1, 2 * i) for i in range(pairs)]
    got = lax.ppermute(other, axis, swap)
    total = mine + got
    carried = jnp.zeros_like(total)
    for hop in range(1, pairs):
        links = [(2 * (hop - 1) + side, 2 * hop + side) for side in range(2)]
        carried = carried + lax.ppermute(carried + total, axis, links)
    first = mine_at == 0
    keep = (carried + jnp.where(first, 0.0, got)).astype(jnp.bfloat16)
    send = (carried + jnp.where(first, mine, 0.0)).astype(jnp.bfloat16)
    back = lax.ppermute(send, axis, swap)
    low = jnp.where(first, keep, back)
    high = jnp.where(first, back, keep)
    return jnp.concatenate([low, high], axis=0)


def shards(query_rows, key_rows, value_rows, gain):
    seq_count, row_count, feat_count = query_rows.shape
    head_size = feat_count // H
    full_gain = lax.all_gather(gain, "dp", axis=0, tiled=True)
    query = query_rows.reshape(row_count, H, head_size)
    keyset = key_rows.reshape(row_count, H, head_size)
    valset = value_rows.reshape(row_count, H, head_size)
    state_terms = jnp.einsum("thd,the->hde", keyset, valset, preferred_element_type=jnp.float32)
    prefix_bf = pair_chain_prefix(state_terms, "ctx")
    causal_mask = jnp.arange(row_count)[:, None] >= jnp.arange(row_count)[None, :]
    scores = jnp.einsum("thd,uhd->htu", query, keyset, preferred_element_type=jnp.float32)
    weights = jnp.where(causal_mask, scores, 0.0).astype(jnp.bfloat16)
    within = jnp.einsum("htu,uhe->the", weights, valset, preferred_element_type=jnp.float32)
    carried = jnp.einsum("thd,hde->the", query, prefix_bf, preferred_element_type=jnp.float32)
    attended = (within + carried).reshape(seq_count, row_count, feat_count)
    scale = lax.rsqrt(jnp.mean(attended * attended, axis=-1, keepdims=True) + 1e-05)
    return (attended * scale * full_gain).astype(jnp.bfloat16)


def solution(mesh):
    in_specs = (
        P(("groups", "dp"), "ctx", None),
        P(("groups", "dp"), "ctx", None),
        P(("groups", "dp"), "ctx", None),
        P("dp"),
    )
    out_specs = P(("groups", "dp"), "ctx", None)
    return jax.shard_map(shards, mesh=mesh, in_specs=in_specs, out_specs=out_specs, check_vma=False)
```

```python
import jax
import jax.numpy as jnp
from jax import lax
from jax.sharding import PartitionSpec as P

H = 32


def pair_chain_prefix(terms, axis, pieces):
    count = lax.axis_size(axis)
    mine_at = lax.axis_index(axis) % 2
    first = mine_at == 0
    half = terms.shape[0] // 2
    pairs = count // 2
    mine_all = lax.dynamic_slice_in_dim(terms, mine_at * half, half, 0)
    other_all = lax.dynamic_slice_in_dim(terms, (1 - mine_at) * half, half, 0)
    swap = [(2 * i, 2 * i + 1) for i in range(pairs)] + [(2 * i + 1, 2 * i) for i in range(pairs)]
    step = half // pieces
    keeps, backs = [], []
    for piece in range(pieces):
        mine = mine_all[piece * step:(piece + 1) * step]
        got = lax.ppermute(other_all[piece * step:(piece + 1) * step], axis, swap)
        total = mine + got
        carried = jnp.zeros_like(total)
        for hop in range(1, pairs):
            links = [(2 * (hop - 1) + side, 2 * hop + side) for side in range(2)]
            carried = carried + lax.ppermute(carried + total, axis, links)
        keeps.append((carried + jnp.where(first, 0.0, got)).astype(jnp.bfloat16))
        send = (carried + jnp.where(first, mine, 0.0)).astype(jnp.bfloat16)
        backs.append(lax.ppermute(send, axis, swap))
    keep = jnp.concatenate(keeps, axis=0)
    back = jnp.concatenate(backs, axis=0)
    low = jnp.where(first, keep, back)
    high = jnp.where(first, back, keep)
    return jnp.concatenate([low, high], axis=0)


def shards(query_rows, key_rows, value_rows, gain):
    seq_count, row_count, feat_count = query_rows.shape
    head_size = feat_count // H
    full_gain = lax.all_gather(gain, "dp", axis=0, tiled=True)
    query = query_rows.reshape(row_count, H, head_size)
    keyset = key_rows.reshape(row_count, H, head_size)
    valset = value_rows.reshape(row_count, H, head_size)
    state_terms = jnp.einsum("thd,the->hde", keyset, valset, preferred_element_type=jnp.float32)
    prefix_bf = pair_chain_prefix(state_terms, "ctx", 4)
    causal_mask = jnp.arange(row_count)[:, None] >= jnp.arange(row_count)[None, :]
    scores = jnp.einsum("thd,uhd->htu", query, keyset, preferred_element_type=jnp.float32)
    weights = jnp.where(causal_mask, scores, 0.0).astype(jnp.bfloat16)
    within = jnp.einsum("htu,uhe->the", weights, valset, preferred_element_type=jnp.float32)
    carried = jnp.einsum("thd,hde->the", query, prefix_bf, preferred_element_type=jnp.float32)
    attended = (within + carried).reshape(seq_count, row_count, feat_count)
    scale = lax.rsqrt(jnp.mean(attended * attended, axis=-1, keepdims=True) + 1e-05)
    return (attended * scale * full_gain).astype(jnp.bfloat16)


def solution(mesh):
    in_specs = (
        P(("groups", "dp"), "ctx", None),
        P(("groups", "dp"), "ctx", None),
        P(("groups", "dp"), "ctx", None),
        P("dp"),
    )
    out_specs = P(("groups", "dp"), "ctx", None)
    return jax.shard_map(shards, mesh=mesh, in_specs=in_specs, out_specs=out_specs, check_vma=False)
```

```python
import jax
import jax.numpy as jnp
from jax import lax
from jax.experimental import pallas as pl
from jax.experimental.pallas import tpu as pltpu
from jax.sharding import PartitionSpec as P

H = 32


def pair_chain_prefix(terms, axis, pieces):
    count = lax.axis_size(axis)
    mine_at = lax.axis_index(axis) % 2
    first = mine_at == 0
    half = terms.shape[0] // 2
    pairs = count // 2
    mine_all = lax.dynamic_slice_in_dim(terms, mine_at * half, half, 0)
    other_all = lax.dynamic_slice_in_dim(terms, (1 - mine_at) * half, half, 0)
    swap = [(2 * i, 2 * i + 1) for i in range(pairs)] + [(2 * i + 1, 2 * i) for i in range(pairs)]
    step = half // pieces
    keeps, backs = [], []
    for piece in range(pieces):
        mine = mine_all[piece * step:(piece + 1) * step]
        got = lax.ppermute(other_all[piece * step:(piece + 1) * step], axis, swap)
        total = mine + got
        carried = jnp.zeros_like(total)
        for hop in range(1, pairs):
            links = [(2 * (hop - 1) + side, 2 * hop + side) for side in range(2)]
            carried = carried + lax.ppermute(carried + total, axis, links)
        keeps.append((carried + jnp.where(first, 0.0, got)).astype(jnp.bfloat16))
        send = (carried + jnp.where(first, mine, 0.0)).astype(jnp.bfloat16)
        backs.append(lax.ppermute(send, axis, swap))
    keep = jnp.concatenate(keeps, axis=0)
    back = jnp.concatenate(backs, axis=0)
    low = jnp.where(first, keep, back)
    high = jnp.where(first, back, keep)
    return jnp.concatenate([low, high], axis=0)


def state_kernel(key_ref, val_ref, out_ref):
    heads, head_size, _ = out_ref.shape
    for head in range(heads):
        cols = slice(head * head_size, (head + 1) * head_size)
        out_ref[head] = lax.dot_general(
            key_ref[:, cols], val_ref[:, cols], (((0,), (0,)), ((), ())),
            preferred_element_type=jnp.float32)


def state_terms_of(keyset, valset, group):
    row_count, feat_count = keyset.shape
    head_size = feat_count // H
    width = group * head_size
    return pl.pallas_call(
        state_kernel,
        grid=(H // group,),
        in_specs=[pl.BlockSpec((row_count, width), lambda g: (0, g)),
                  pl.BlockSpec((row_count, width), lambda g: (0, g))],
        out_specs=pl.BlockSpec((group, head_size, head_size), lambda g: (g, 0, 0)),
        out_shape=jax.ShapeDtypeStruct((H, head_size, head_size), jnp.float32),
    )(keyset, valset)


def attend_kernel(query_ref, key_ref, val_ref, prefix_ref, gain_ref, out_ref, acc_ref, sumsq_ref):
    step = pl.program_id(0)
    row_count, width = query_ref.shape
    heads, head_size, _ = prefix_ref.shape
    causal = (lax.broadcasted_iota(jnp.int32, (row_count, row_count), 0)
              >= lax.broadcasted_iota(jnp.int32, (row_count, row_count), 1))

    @pl.when(step == 0)
    def _():
        sumsq_ref[...] = jnp.zeros_like(sumsq_ref)

    sumsq = sumsq_ref[...]
    for head in range(heads):
        cols = slice(head * head_size, (head + 1) * head_size)
        query = query_ref[:, cols]
        scores = lax.dot_general(query, key_ref[:, cols], (((1,), (1,)), ((), ())),
                                 preferred_element_type=jnp.float32)
        weights = jnp.where(causal, scores, 0.0).astype(jnp.bfloat16)
        within = jnp.dot(weights, val_ref[:, cols], preferred_element_type=jnp.float32)
        carried = jnp.dot(query, prefix_ref[head], preferred_element_type=jnp.float32)
        attended = within + carried
        acc_ref[step, :, cols] = attended
        sumsq = sumsq + jnp.sum(attended * attended, axis=1, keepdims=True)
    sumsq_ref[...] = sumsq

    @pl.when(step == pl.num_programs(0) - 1)
    def _():
        scale = lax.rsqrt(sumsq / (width * pl.num_programs(0)) + 1e-05)
        for part in range(acc_ref.shape[0]):
            cols = slice(part * width, (part + 1) * width)
            out_ref[:, cols] = (acc_ref[part] * scale * gain_ref[:, cols]).astype(out_ref.dtype)


def attend_of(query, keyset, valset, prefix_bf, full_gain, group):
    row_count, feat_count = query.shape
    head_size = feat_count // H
    width = group * head_size
    steps = H // group
    return pl.pallas_call(
        attend_kernel,
        grid=(steps,),
        in_specs=[pl.BlockSpec((row_count, width), lambda g: (0, g)),
                  pl.BlockSpec((row_count, width), lambda g: (0, g)),
                  pl.BlockSpec((row_count, width), lambda g: (0, g)),
                  pl.BlockSpec((group, head_size, head_size), lambda g: (g, 0, 0)),
                  pl.BlockSpec((1, feat_count), lambda g: (0, 0))],
        out_specs=pl.BlockSpec((row_count, feat_count), lambda g: (0, 0)),
        out_shape=jax.ShapeDtypeStruct((row_count, feat_count), jnp.bfloat16),
        scratch_shapes=[pltpu.VMEM((steps, row_count, width), jnp.float32),
                        pltpu.VMEM((row_count, 1), jnp.float32)],
    )(query, keyset, valset, prefix_bf, full_gain)


def shards(query_rows, key_rows, value_rows, gain):
    seq_count, row_count, feat_count = query_rows.shape
    full_gain = lax.all_gather(gain, "dp", axis=0, tiled=True).reshape(1, feat_count)
    query = query_rows.reshape(seq_count * row_count, feat_count)
    keyset = key_rows.reshape(seq_count * row_count, feat_count)
    valset = value_rows.reshape(seq_count * row_count, feat_count)
    state_terms = state_terms_of(keyset, valset, 8)
    prefix_bf = pair_chain_prefix(state_terms, "ctx", 4)
    normed = attend_of(query, keyset, valset, prefix_bf, full_gain, 8)
    return normed.reshape(seq_count, row_count, feat_count)


def solution(mesh):
    in_specs = (
        P(("groups", "dp"), "ctx", None),
        P(("groups", "dp"), "ctx", None),
        P(("groups", "dp"), "ctx", None),
        P("dp"),
    )
    out_specs = P(("groups", "dp"), "ctx", None)
    return jax.shard_map(shards, mesh=mesh, in_specs=in_specs, out_specs=out_specs, check_vma=False)
```

```python
import jax
import jax.numpy as jnp
from jax import lax
from jax.experimental import pallas as pl
from jax.experimental.pallas import tpu as pltpu
from jax.sharding import PartitionSpec as P

H = 32


def pair_chain_prefix(terms, axis, pieces):
    count = lax.axis_size(axis)
    place = lax.axis_index(axis)
    side = place % 2
    level = place // 2
    first = side == 0
    half = terms.shape[0] // 2
    levels = count // 2
    shape = (pieces, half // pieces) + terms.shape[1:]
    mine_all = lax.dynamic_slice_in_dim(terms, side * half, half, 0).reshape(shape)
    other_all = lax.dynamic_slice_in_dim(terms, (1 - side) * half, half, 0).reshape(shape)

    def swap_at(at):
        return [(2 * lv, 2 * lv + 1) for lv in at] + [(2 * lv + 1, 2 * lv) for lv in at]

    def put(buffer, index, valid, value):
        value = jnp.where(valid, value, lax.dynamic_index_in_dim(buffer, index, 0, keepdims=False))
        return lax.dynamic_update_index_in_dim(buffer, value, index, 0)

    got_all = jnp.zeros_like(mine_all)
    carried_all = jnp.zeros_like(mine_all)
    keep_all = jnp.zeros(shape, jnp.bfloat16)
    back_all = jnp.zeros(shape, jnp.bfloat16)
    for t in range(pieces + levels - 1):
        if t < pieces:
            got_all = got_all.at[t].set(lax.ppermute(other_all[t], axis, swap_at(range(levels))))
        active = [lv for lv in range(levels) if 0 <= t - lv < pieces]
        piece = jnp.clip(t - level, 0, pieces - 1)
        valid = (t - level >= 0) & (t - level < pieces)
        carried = lax.dynamic_index_in_dim(carried_all, piece, 0, keepdims=False)
        mine = lax.dynamic_index_in_dim(mine_all, piece, 0, keepdims=False)
        got = lax.dynamic_index_in_dim(got_all, piece, 0, keepdims=False)
        links = [(2 * lv + s, 2 * (lv + 1) + s) for lv in active if lv + 1 < levels for s in range(2)]
        if links:
            came = lax.ppermute(carried + mine + got, axis, links)
            arrived = t - level + 1
            came_ok = (arrived >= 0) & (arrived < pieces) & (level >= 1)
            carried_all = put(carried_all, jnp.clip(arrived, 0, pieces - 1), came_ok, came)
        keep = (carried + jnp.where(first, 0.0, got)).astype(jnp.bfloat16)
        send = (carried + jnp.where(first, mine, 0.0)).astype(jnp.bfloat16)
        back = lax.ppermute(send, axis, swap_at(active))
        keep_all = put(keep_all, piece, valid, keep)
        back_all = put(back_all, piece, valid, back)
    keep = keep_all.reshape((half,) + terms.shape[1:])
    back = back_all.reshape((half,) + terms.shape[1:])
    low = jnp.where(first, keep, back)
    high = jnp.where(first, back, keep)
    return jnp.concatenate([low, high], axis=0)


def state_kernel(key_ref, val_ref, out_ref):
    heads, head_size, _ = out_ref.shape
    for head in range(heads):
        cols = slice(head * head_size, (head + 1) * head_size)
        out_ref[head] = lax.dot_general(
            key_ref[:, cols], val_ref[:, cols], (((0,), (0,)), ((), ())),
            preferred_element_type=jnp.float32)


def state_terms_of(keyset, valset, group):
    row_count, feat_count = keyset.shape
    head_size = feat_count // H
    width = group * head_size
    return pl.pallas_call(
        state_kernel,
        grid=(H // group,),
        in_specs=[pl.BlockSpec((row_count, width), lambda g: (0, g)),
                  pl.BlockSpec((row_count, width), lambda g: (0, g))],
        out_specs=pl.BlockSpec((group, head_size, head_size), lambda g: (g, 0, 0)),
        out_shape=jax.ShapeDtypeStruct((H, head_size, head_size), jnp.float32),
    )(keyset, valset)


def attend_kernel(query_ref, key_ref, val_ref, prefix_ref, gain_ref, out_ref, acc_ref, sumsq_ref):
    step = pl.program_id(0)
    row_count, width = query_ref.shape
    heads, head_size, _ = prefix_ref.shape
    causal = (lax.broadcasted_iota(jnp.int32, (row_count, row_count), 0)
              >= lax.broadcasted_iota(jnp.int32, (row_count, row_count), 1))

    @pl.when(step == 0)
    def _():
        sumsq_ref[...] = jnp.zeros_like(sumsq_ref)

    sumsq = sumsq_ref[...]
    for head in range(heads):
        cols = slice(head * head_size, (head + 1) * head_size)
        query = query_ref[:, cols]
        scores = lax.dot_general(query, key_ref[:, cols], (((1,), (1,)), ((), ())),
                                 preferred_element_type=jnp.float32)
        weights = jnp.where(causal, scores, 0.0).astype(jnp.bfloat16)
        within = jnp.dot(weights, val_ref[:, cols], preferred_element_type=jnp.float32)
        carried = jnp.dot(query, prefix_ref[head], preferred_element_type=jnp.float32)
        attended = within + carried
        acc_ref[step, :, cols] = attended
        sumsq = sumsq + jnp.sum(attended * attended, axis=1, keepdims=True)
    sumsq_ref[...] = sumsq

    @pl.when(step == pl.num_programs(0) - 1)
    def _():
        scale = lax.rsqrt(sumsq / (width * pl.num_programs(0)) + 1e-05)
        for part in range(acc_ref.shape[0]):
            cols = slice(part * width, (part + 1) * width)
            out_ref[:, cols] = (acc_ref[part] * scale * gain_ref[:, cols]).astype(out_ref.dtype)


def attend_of(query, keyset, valset, prefix_bf, full_gain, group):
    row_count, feat_count = query.shape
    head_size = feat_count // H
    width = group * head_size
    steps = H // group
    return pl.pallas_call(
        attend_kernel,
        grid=(steps,),
        in_specs=[pl.BlockSpec((row_count, width), lambda g: (0, g)),
                  pl.BlockSpec((row_count, width), lambda g: (0, g)),
                  pl.BlockSpec((row_count, width), lambda g: (0, g)),
                  pl.BlockSpec((group, head_size, head_size), lambda g: (g, 0, 0)),
                  pl.BlockSpec((1, feat_count), lambda g: (0, 0))],
        out_specs=pl.BlockSpec((row_count, feat_count), lambda g: (0, 0)),
        out_shape=jax.ShapeDtypeStruct((row_count, feat_count), jnp.bfloat16),
        scratch_shapes=[pltpu.VMEM((steps, row_count, width), jnp.float32),
                        pltpu.VMEM((row_count, 1), jnp.float32)],
    )(query, keyset, valset, prefix_bf, full_gain)


def shards(query_rows, key_rows, value_rows, gain):
    seq_count, row_count, feat_count = query_rows.shape
    full_gain = lax.all_gather(gain, "dp", axis=0, tiled=True).reshape(1, feat_count)
    query = query_rows.reshape(seq_count * row_count, feat_count)
    keyset = key_rows.reshape(seq_count * row_count, feat_count)
    valset = value_rows.reshape(seq_count * row_count, feat_count)
    state_terms = state_terms_of(keyset, valset, 8)
    prefix_bf = pair_chain_prefix(state_terms, "ctx", 4)
    normed = attend_of(query, keyset, valset, prefix_bf, full_gain, 8)
    return normed.reshape(seq_count, row_count, feat_count)


def solution(mesh):
    in_specs = (
        P(("groups", "dp"), "ctx", None),
        P(("groups", "dp"), "ctx", None),
        P(("groups", "dp"), "ctx", None),
        P("dp"),
    )
    out_specs = P(("groups", "dp"), "ctx", None)
    return jax.shard_map(shards, mesh=mesh, in_specs=in_specs, out_specs=out_specs, check_vma=False)
```

```python
import functools

import jax
import jax.numpy as jnp
from jax import lax
from jax.experimental import pallas as pl
from jax.experimental.pallas import tpu as pltpu
from jax.sharding import PartitionSpec as P

H = 32


def pair_chain_prefix(terms, axis, pieces):
    count = lax.axis_size(axis)
    mine_at = lax.axis_index(axis) % 2
    first = mine_at == 0
    half = terms.shape[0] // 2
    pairs = count // 2
    mine_all = lax.dynamic_slice_in_dim(terms, mine_at * half, half, 0)
    other_all = lax.dynamic_slice_in_dim(terms, (1 - mine_at) * half, half, 0)
    swap = [(2 * i, 2 * i + 1) for i in range(pairs)] + [(2 * i + 1, 2 * i) for i in range(pairs)]
    step = half // pieces
    keeps, backs = [], []
    for piece in range(pieces):
        mine = mine_all[piece * step:(piece + 1) * step]
        got = lax.ppermute(other_all[piece * step:(piece + 1) * step], axis, swap)
        total = mine + got
        carried = jnp.zeros_like(total)
        for hop in range(1, pairs):
            links = [(2 * (hop - 1) + side, 2 * hop + side) for side in range(2)]
            carried = carried + lax.ppermute(carried + total, axis, links)
        keeps.append((carried + jnp.where(first, 0.0, got)).astype(jnp.bfloat16))
        send = (carried + jnp.where(first, mine, 0.0)).astype(jnp.bfloat16)
        backs.append(lax.ppermute(send, axis, swap))
    keep = jnp.concatenate(keeps, axis=0)
    back = jnp.concatenate(backs, axis=0)
    low = jnp.where(first, keep, back)
    high = jnp.where(first, back, keep)
    return jnp.concatenate([low, high], axis=0)


def state_kernel(key_ref, val_ref, out_ref):
    heads, head_size, _ = out_ref.shape
    for head in range(heads):
        cols = slice(head * head_size, (head + 1) * head_size)
        out_ref[head] = lax.dot_general(
            key_ref[:, cols], val_ref[:, cols], (((0,), (0,)), ((), ())),
            preferred_element_type=jnp.float32)


def state_terms_of(keyset, valset, group):
    row_count, feat_count = keyset.shape
    head_size = feat_count // H
    width = group * head_size
    return pl.pallas_call(
        state_kernel,
        grid=(H // group,),
        in_specs=[pl.BlockSpec((row_count, width), lambda g: (0, g)),
                  pl.BlockSpec((row_count, width), lambda g: (0, g))],
        out_specs=pl.BlockSpec((group, head_size, head_size), lambda g: (g, 0, 0)),
        out_shape=jax.ShapeDtypeStruct((H, head_size, head_size), jnp.float32),
    )(keyset, valset)


def within_kernel(head_size, query_ref, key_ref, val_ref, out_ref):
    row_count, width = query_ref.shape
    causal = (lax.broadcasted_iota(jnp.int32, (row_count, row_count), 0)
              >= lax.broadcasted_iota(jnp.int32, (row_count, row_count), 1))
    for head in range(width // head_size):
        cols = slice(head * head_size, (head + 1) * head_size)
        scores = lax.dot_general(query_ref[:, cols], key_ref[:, cols], (((1,), (1,)), ((), ())),
                                 preferred_element_type=jnp.float32)
        weights = jnp.where(causal, scores, 0.0).astype(jnp.bfloat16)
        out_ref[:, cols] = jnp.dot(weights, val_ref[:, cols], preferred_element_type=jnp.float32)


def within_of(query, keyset, valset, group):
    row_count, feat_count = query.shape
    width = group * (feat_count // H)
    spec = pl.BlockSpec((row_count, width), lambda g: (0, g))
    return pl.pallas_call(
        functools.partial(within_kernel, feat_count // H),
        grid=(H // group,),
        in_specs=[spec, spec, spec],
        out_specs=spec,
        out_shape=jax.ShapeDtypeStruct((row_count, feat_count), jnp.float32),
    )(query, keyset, valset)


def finish_kernel(query_ref, within_ref, prefix_ref, gain_ref, out_ref, acc_ref, sumsq_ref):
    step = pl.program_id(0)
    row_count, width = query_ref.shape
    heads, head_size, _ = prefix_ref.shape

    @pl.when(step == 0)
    def _():
        sumsq_ref[...] = jnp.zeros_like(sumsq_ref)

    sumsq = sumsq_ref[...]
    for head in range(heads):
        cols = slice(head * head_size, (head + 1) * head_size)
        carried = jnp.dot(query_ref[:, cols], prefix_ref[head], preferred_element_type=jnp.float32)
        attended = within_ref[:, cols] + carried
        acc_ref[step, :, cols] = attended
        sumsq = sumsq + jnp.sum(attended * attended, axis=1, keepdims=True)
    sumsq_ref[...] = sumsq

    @pl.when(step == pl.num_programs(0) - 1)
    def _():
        scale = lax.rsqrt(sumsq / (width * pl.num_programs(0)) + 1e-05)
        for part in range(acc_ref.shape[0]):
            cols = slice(part * width, (part + 1) * width)
            out_ref[:, cols] = (acc_ref[part] * scale * gain_ref[:, cols]).astype(out_ref.dtype)


def finish_of(query, within, prefix_bf, full_gain, group):
    row_count, feat_count = query.shape
    head_size = feat_count // H
    width = group * head_size
    steps = H // group
    spec = pl.BlockSpec((row_count, width), lambda g: (0, g))
    return pl.pallas_call(
        finish_kernel,
        grid=(steps,),
        in_specs=[spec, spec,
                  pl.BlockSpec((group, head_size, head_size), lambda g: (g, 0, 0)),
                  pl.BlockSpec((1, feat_count), lambda g: (0, 0))],
        out_specs=pl.BlockSpec((row_count, feat_count), lambda g: (0, 0)),
        out_shape=jax.ShapeDtypeStruct((row_count, feat_count), jnp.bfloat16),
        scratch_shapes=[pltpu.VMEM((steps, row_count, width), jnp.float32),
                        pltpu.VMEM((row_count, 1), jnp.float32)],
    )(query, within, prefix_bf, full_gain)


def shards(query_rows, key_rows, value_rows, gain):
    seq_count, row_count, feat_count = query_rows.shape
    full_gain = lax.all_gather(gain, "dp", axis=0, tiled=True).reshape(1, feat_count)
    query = query_rows.reshape(seq_count * row_count, feat_count)
    keyset = key_rows.reshape(seq_count * row_count, feat_count)
    valset = value_rows.reshape(seq_count * row_count, feat_count)
    state_terms = state_terms_of(keyset, valset, 8)
    prefix_bf = pair_chain_prefix(state_terms, "ctx", 4)
    within = within_of(query, keyset, valset, 8)
    normed = finish_of(query, within, prefix_bf, full_gain, 8)
    return normed.reshape(seq_count, row_count, feat_count)


def solution(mesh):
    in_specs = (
        P(("groups", "dp"), "ctx", None),
        P(("groups", "dp"), "ctx", None),
        P(("groups", "dp"), "ctx", None),
        P("dp"),
    )
    out_specs = P(("groups", "dp"), "ctx", None)
    return jax.shard_map(shards, mesh=mesh, in_specs=in_specs, out_specs=out_specs, check_vma=False)
```

```python
import jax
import jax.numpy as jnp
from jax import lax
from jax.experimental import pallas as pl
from jax.experimental.pallas import tpu as pltpu
from jax.sharding import PartitionSpec as P

H = 32


def pair_chain_prefix(terms, axis, pieces):
    count = lax.axis_size(axis)
    mine_at = lax.axis_index(axis) % 2
    first = mine_at == 0
    half = terms.shape[0] // 2
    pairs = count // 2
    mine_all = lax.dynamic_slice_in_dim(terms, mine_at * half, half, 0)
    other_all = lax.dynamic_slice_in_dim(terms, (1 - mine_at) * half, half, 0)
    swap = [(2 * i, 2 * i + 1) for i in range(pairs)] + [(2 * i + 1, 2 * i) for i in range(pairs)]
    got_all = lax.ppermute(other_all, axis, swap)
    step = half // pieces
    keeps, backs = [], []
    for piece in range(pieces):
        mine = mine_all[piece * step:(piece + 1) * step]
        got = got_all[piece * step:(piece + 1) * step]
        total = mine + got
        carried = jnp.zeros_like(total)
        for hop in range(1, pairs):
            links = [(2 * (hop - 1) + side, 2 * hop + side) for side in range(2)]
            send = carried + total
            if hop == pairs - 1 and piece >= 2:
                send, _ = lax.optimization_barrier((send, backs[piece - 2]))
            carried = carried + lax.ppermute(send, axis, links)
        keeps.append((carried + jnp.where(first, 0.0, got)).astype(jnp.bfloat16))
        send = (carried + jnp.where(first, mine, 0.0)).astype(jnp.bfloat16)
        backs.append(lax.ppermute(send, axis, swap))
    keep = jnp.concatenate(keeps, axis=0)
    back = jnp.concatenate(backs, axis=0)
    low = jnp.where(first, keep, back)
    high = jnp.where(first, back, keep)
    return jnp.concatenate([low, high], axis=0)


def state_kernel(key_ref, val_ref, out_ref):
    heads, head_size, _ = out_ref.shape
    for head in range(heads):
        cols = slice(head * head_size, (head + 1) * head_size)
        out_ref[head] = lax.dot_general(
            key_ref[:, cols], val_ref[:, cols], (((0,), (0,)), ((), ())),
            preferred_element_type=jnp.float32)


def state_terms_of(keyset, valset, group):
    row_count, feat_count = keyset.shape
    head_size = feat_count // H
    width = group * head_size
    return pl.pallas_call(
        state_kernel,
        grid=(H // group,),
        in_specs=[pl.BlockSpec((row_count, width), lambda g: (0, g)),
                  pl.BlockSpec((row_count, width), lambda g: (0, g))],
        out_specs=pl.BlockSpec((group, head_size, head_size), lambda g: (g, 0, 0)),
        out_shape=jax.ShapeDtypeStruct((H, head_size, head_size), jnp.float32),
    )(keyset, valset)


def attend_kernel(query_ref, key_ref, val_ref, prefix_ref, gain_ref, out_ref, acc_ref, sumsq_ref):
    step = pl.program_id(0)
    row_count, width = query_ref.shape
    heads, head_size, _ = prefix_ref.shape
    causal = (lax.broadcasted_iota(jnp.int32, (row_count, row_count), 0)
              >= lax.broadcasted_iota(jnp.int32, (row_count, row_count), 1))

    @pl.when(step == 0)
    def _():
        sumsq_ref[...] = jnp.zeros_like(sumsq_ref)

    sumsq = sumsq_ref[...]
    for head in range(heads):
        cols = slice(head * head_size, (head + 1) * head_size)
        query = query_ref[:, cols]
        scores = lax.dot_general(query, key_ref[:, cols], (((1,), (1,)), ((), ())),
                                 preferred_element_type=jnp.float32)
        weights = jnp.where(causal, scores, 0.0).astype(jnp.bfloat16)
        within = jnp.dot(weights, val_ref[:, cols], preferred_element_type=jnp.float32)
        carried = jnp.dot(query, prefix_ref[head], preferred_element_type=jnp.float32)
        attended = within + carried
        acc_ref[step, :, cols] = attended
        sumsq = sumsq + jnp.sum(attended * attended, axis=1, keepdims=True)
    sumsq_ref[...] = sumsq

    @pl.when(step == pl.num_programs(0) - 1)
    def _():
        scale = lax.rsqrt(sumsq / (width * pl.num_programs(0)) + 1e-05)
        for part in range(acc_ref.shape[0]):
            cols = slice(part * width, (part + 1) * width)
            out_ref[:, cols] = (acc_ref[part] * scale * gain_ref[:, cols]).astype(out_ref.dtype)


def attend_of(query, keyset, valset, prefix_bf, full_gain, group):
    row_count, feat_count = query.shape
    head_size = feat_count // H
    width = group * head_size
    steps = H // group
    return pl.pallas_call(
        attend_kernel,
        grid=(steps,),
        in_specs=[pl.BlockSpec((row_count, width), lambda g: (0, g)),
                  pl.BlockSpec((row_count, width), lambda g: (0, g)),
                  pl.BlockSpec((row_count, width), lambda g: (0, g)),
                  pl.BlockSpec((group, head_size, head_size), lambda g: (g, 0, 0)),
                  pl.BlockSpec((1, feat_count), lambda g: (0, 0))],
        out_specs=pl.BlockSpec((row_count, feat_count), lambda g: (0, 0)),
        out_shape=jax.ShapeDtypeStruct((row_count, feat_count), jnp.bfloat16),
        scratch_shapes=[pltpu.VMEM((steps, row_count, width), jnp.float32),
                        pltpu.VMEM((row_count, 1), jnp.float32)],
    )(query, keyset, valset, prefix_bf, full_gain)


def shards(query_rows, key_rows, value_rows, gain):
    seq_count, row_count, feat_count = query_rows.shape
    full_gain = lax.all_gather(gain, "dp", axis=0, tiled=True).reshape(1, feat_count)
    query = query_rows.reshape(seq_count * row_count, feat_count)
    keyset = key_rows.reshape(seq_count * row_count, feat_count)
    valset = value_rows.reshape(seq_count * row_count, feat_count)
    state_terms = state_terms_of(keyset, valset, 8)
    prefix_bf = pair_chain_prefix(state_terms, "ctx", 4)
    normed = attend_of(query, keyset, valset, prefix_bf, full_gain, 8)
    return normed.reshape(seq_count, row_count, feat_count)


def solution(mesh):
    in_specs = (
        P(("groups", "dp"), "ctx", None),
        P(("groups", "dp"), "ctx", None),
        P(("groups", "dp"), "ctx", None),
        P("dp"),
    )
    out_specs = P(("groups", "dp"), "ctx", None)
    return jax.shard_map(shards, mesh=mesh, in_specs=in_specs, out_specs=out_specs, check_vma=False)
```

```python
import jax
import jax.numpy as jnp
from jax import lax
from jax.experimental import pallas as pl
from jax.experimental.pallas import tpu as pltpu
from jax.sharding import PartitionSpec as P

H = 32


def pair_chain_prefix(mine_all, other_all, axis, pieces):
    count = lax.axis_size(axis)
    mine_at = lax.axis_index(axis) % 2
    first = mine_at == 0
    half = mine_all.shape[0]
    pairs = count // 2
    swap = [(2 * i, 2 * i + 1) for i in range(pairs)] + [(2 * i + 1, 2 * i) for i in range(pairs)]
    step = half // pieces
    keeps, backs = [], []
    for piece in range(pieces):
        mine = mine_all[piece * step:(piece + 1) * step]
        got = lax.ppermute(other_all[piece * step:(piece + 1) * step], axis, swap)
        total = mine + got
        carried = jnp.zeros_like(total)
        for hop in range(1, pairs):
            links = [(2 * (hop - 1) + side, 2 * hop + side) for side in range(2)]
            carried = carried + lax.ppermute(carried + total, axis, links)
        keeps.append((carried + jnp.where(first, 0.0, got)).astype(jnp.bfloat16))
        send = (carried + jnp.where(first, mine, 0.0)).astype(jnp.bfloat16)
        backs.append(lax.ppermute(send, axis, swap))
    keep = jnp.concatenate(keeps, axis=0)
    back = jnp.concatenate(backs, axis=0)
    low = jnp.where(first, keep, back)
    high = jnp.where(first, back, keep)
    return jnp.concatenate([low, high], axis=0)


def state_kernel(at_ref, key_ref, val_ref, out_ref):
    heads, head_size, _ = out_ref.shape
    for head in range(heads):
        cols = slice(head * head_size, (head + 1) * head_size)
        out_ref[head] = lax.dot_general(
            key_ref[:, cols], val_ref[:, cols], (((0,), (0,)), ((), ())),
            preferred_element_type=jnp.float32)


def state_terms_of(keyset, valset, half_at):
    row_count, feat_count = keyset.shape
    head_size = feat_count // H
    width = feat_count // 2
    spec = pl.BlockSpec((row_count, width), lambda g, at: (0, at[0] + g))
    return pl.pallas_call(
        state_kernel,
        grid_spec=pltpu.PrefetchScalarGridSpec(
            num_scalar_prefetch=1,
            grid=(1,),
            in_specs=[spec, spec],
            out_specs=pl.BlockSpec((H // 2, head_size, head_size), lambda g, at: (0, 0, 0))),
        out_shape=jax.ShapeDtypeStruct((H // 2, head_size, head_size), jnp.float32),
    )(jnp.reshape(half_at, (1,)).astype(jnp.int32), keyset, valset)


def attend_kernel(query_ref, key_ref, val_ref, prefix_ref, gain_ref, out_ref, acc_ref, sumsq_ref):
    step = pl.program_id(0)
    row_count, width = query_ref.shape
    heads, head_size, _ = prefix_ref.shape
    causal = (lax.broadcasted_iota(jnp.int32, (row_count, row_count), 0)
              >= lax.broadcasted_iota(jnp.int32, (row_count, row_count), 1))

    @pl.when(step == 0)
    def _():
        sumsq_ref[...] = jnp.zeros_like(sumsq_ref)

    sumsq = sumsq_ref[...]
    for head in range(heads):
        cols = slice(head * head_size, (head + 1) * head_size)
        query = query_ref[:, cols]
        scores = lax.dot_general(query, key_ref[:, cols], (((1,), (1,)), ((), ())),
                                 preferred_element_type=jnp.float32)
        weights = jnp.where(causal, scores, 0.0).astype(jnp.bfloat16)
        within = jnp.dot(weights, val_ref[:, cols], preferred_element_type=jnp.float32)
        carried = jnp.dot(query, prefix_ref[head], preferred_element_type=jnp.float32)
        attended = within + carried
        acc_ref[step, :, cols] = attended
        sumsq = sumsq + jnp.sum(attended * attended, axis=1, keepdims=True)
    sumsq_ref[...] = sumsq

    @pl.when(step == pl.num_programs(0) - 1)
    def _():
        scale = lax.rsqrt(sumsq / (width * pl.num_programs(0)) + 1e-05)
        for part in range(acc_ref.shape[0]):
            cols = slice(part * width, (part + 1) * width)
            out_ref[:, cols] = (acc_ref[part] * scale * gain_ref[:, cols]).astype(out_ref.dtype)


def attend_of(query, keyset, valset, prefix_bf, full_gain, group):
    row_count, feat_count = query.shape
    head_size = feat_count // H
    width = group * head_size
    steps = H // group
    return pl.pallas_call(
        attend_kernel,
        grid=(steps,),
        in_specs=[pl.BlockSpec((row_count, width), lambda g: (0, g)),
                  pl.BlockSpec((row_count, width), lambda g: (0, g)),
                  pl.BlockSpec((row_count, width), lambda g: (0, g)),
                  pl.BlockSpec((group, head_size, head_size), lambda g: (g, 0, 0)),
                  pl.BlockSpec((1, feat_count), lambda g: (0, 0))],
        out_specs=pl.BlockSpec((row_count, feat_count), lambda g: (0, 0)),
        out_shape=jax.ShapeDtypeStruct((row_count, feat_count), jnp.bfloat16),
        scratch_shapes=[pltpu.VMEM((steps, row_count, width), jnp.float32),
                        pltpu.VMEM((row_count, 1), jnp.float32)],
    )(query, keyset, valset, prefix_bf, full_gain)


def shards(query_rows, key_rows, value_rows, gain):
    seq_count, row_count, feat_count = query_rows.shape
    full_gain = lax.all_gather(gain, "dp", axis=0, tiled=True).reshape(1, feat_count)
    query = query_rows.reshape(seq_count * row_count, feat_count)
    keyset = key_rows.reshape(seq_count * row_count, feat_count)
    valset = value_rows.reshape(seq_count * row_count, feat_count)
    mine_at = lax.axis_index("ctx") % 2
    other_terms = state_terms_of(keyset, valset, 1 - mine_at)
    mine_terms = state_terms_of(keyset, valset, mine_at)
    prefix_bf = pair_chain_prefix(mine_terms, other_terms, "ctx", 4)
    normed = attend_of(query, keyset, valset, prefix_bf, full_gain, 8)
    return normed.reshape(seq_count, row_count, feat_count)


def solution(mesh):
    in_specs = (
        P(("groups", "dp"), "ctx", None),
        P(("groups", "dp"), "ctx", None),
        P(("groups", "dp"), "ctx", None),
        P("dp"),
    )
    out_specs = P(("groups", "dp"), "ctx", None)
    return jax.shard_map(shards, mesh=mesh, in_specs=in_specs, out_specs=out_specs, check_vma=False)
```

```python
import jax
import jax.numpy as jnp
from jax import lax
from jax.experimental import pallas as pl
from jax.experimental.pallas import tpu as pltpu
from jax.sharding import PartitionSpec as P

H = 32


def pair_chain_prefix(terms, axis, pieces):
    count = lax.axis_size(axis)
    mine_at = lax.axis_index(axis) % 2
    first = mine_at == 0
    half = terms.shape[0] // 2
    pairs = count // 2
    mine_all = lax.dynamic_slice_in_dim(terms, mine_at * half, half, 0)
    other_all = lax.dynamic_slice_in_dim(terms, (1 - mine_at) * half, half, 0)
    swap = [(2 * i, 2 * i + 1) for i in range(pairs)] + [(2 * i + 1, 2 * i) for i in range(pairs)]
    step = half // pieces
    keeps, backs = [], []
    for piece in range(pieces):
        mine = mine_all[piece * step:(piece + 1) * step]
        got = lax.ppermute(other_all[piece * step:(piece + 1) * step], axis, swap)
        total = mine + got
        carried = jnp.zeros_like(total)
        for hop in range(1, pairs):
            links = [(2 * (hop - 1) + side, 2 * hop + side) for side in range(2)]
            carried = carried + lax.ppermute(carried + total, axis, links)
        keeps.append((carried + jnp.where(first, 0.0, got)).astype(jnp.bfloat16))
        send = (carried + jnp.where(first, mine, 0.0)).astype(jnp.bfloat16)
        backs.append(lax.ppermute(send, axis, swap))
    keep = jnp.concatenate(keeps, axis=0)
    back = jnp.concatenate(backs, axis=0)
    low = jnp.where(first, keep, back)
    high = jnp.where(first, back, keep)
    return jnp.concatenate([low, high], axis=0)


def state_kernel(key_ref, val_ref, out_ref):
    heads, head_size, _ = out_ref.shape
    for head in range(heads):
        cols = slice(head * head_size, (head + 1) * head_size)
        out_ref[head] = lax.dot_general(
            key_ref[:, cols], val_ref[:, cols], (((0,), (0,)), ((), ())),
            preferred_element_type=jnp.float32)


def state_terms_of(keyset, valset, group):
    row_count, feat_count = keyset.shape
    head_size = feat_count // H
    width = group * head_size
    return pl.pallas_call(
        state_kernel,
        grid=(H // group,),
        in_specs=[pl.BlockSpec((row_count, width), lambda g: (0, g)),
                  pl.BlockSpec((row_count, width), lambda g: (0, g))],
        out_specs=pl.BlockSpec((group, head_size, head_size), lambda g: (g, 0, 0)),
        out_shape=jax.ShapeDtypeStruct((H, head_size, head_size), jnp.float32),
    )(keyset, valset)


def attend_kernel(query_ref, key_ref, val_ref, prefix_ref, gain_ref, out_ref, acc_ref, sumsq_ref):
    step = pl.program_id(0)
    row_count, width = query_ref.shape
    heads, head_size, _ = prefix_ref.shape
    causal = (lax.broadcasted_iota(jnp.int32, (row_count, row_count), 0)
              >= lax.broadcasted_iota(jnp.int32, (row_count, row_count), 1))

    @pl.when(step == 0)
    def _():
        sumsq_ref[...] = jnp.zeros_like(sumsq_ref)

    sumsq = sumsq_ref[...]
    for head in range(heads):
        cols = slice(head * head_size, (head + 1) * head_size)
        query = query_ref[:, cols]
        scores = lax.dot_general(query, key_ref[:, cols], (((1,), (1,)), ((), ())),
                                 preferred_element_type=jnp.float32)
        weights = jnp.where(causal, scores, 0.0).astype(jnp.bfloat16)
        within = jnp.dot(weights, val_ref[:, cols], preferred_element_type=jnp.float32)
        carried = jnp.dot(query, prefix_ref[head], preferred_element_type=jnp.float32)
        attended = within + carried
        acc_ref[step, :, cols] = attended
        sumsq = sumsq + jnp.sum(attended * attended, axis=1, keepdims=True)
    sumsq_ref[...] = sumsq

    @pl.when(step == pl.num_programs(0) - 1)
    def _():
        scale = lax.rsqrt(sumsq / (width * pl.num_programs(0)) + 1e-05)
        for part in range(acc_ref.shape[0]):
            cols = slice(part * width, (part + 1) * width)
            out_ref[:, cols] = (acc_ref[part] * scale * gain_ref[:, cols]).astype(out_ref.dtype)


def attend_of(query, keyset, valset, prefix_bf, full_gain, group):
    row_count, feat_count = query.shape
    head_size = feat_count // H
    width = group * head_size
    steps = H // group
    return pl.pallas_call(
        attend_kernel,
        grid=(steps,),
        in_specs=[pl.BlockSpec((row_count, width), lambda g: (0, g)),
                  pl.BlockSpec((row_count, width), lambda g: (0, g)),
                  pl.BlockSpec((row_count, width), lambda g: (0, g)),
                  pl.BlockSpec((group, head_size, head_size), lambda g: (g, 0, 0)),
                  pl.BlockSpec((1, feat_count), lambda g: (0, 0))],
        out_specs=pl.BlockSpec((row_count, feat_count), lambda g: (0, 0)),
        out_shape=jax.ShapeDtypeStruct((row_count, feat_count), jnp.bfloat16),
        scratch_shapes=[pltpu.VMEM((steps, row_count, width), jnp.float32),
                        pltpu.VMEM((row_count, 1), jnp.float32)],
    )(query, keyset, valset, prefix_bf, full_gain)


def shards(query_rows, key_rows, value_rows, gain):
    seq_count, row_count, feat_count = query_rows.shape
    full_gain = lax.all_gather(gain, "dp", axis=0, tiled=True).reshape(1, feat_count)
    query = query_rows.reshape(seq_count * row_count, feat_count)
    keyset = key_rows.reshape(seq_count * row_count, feat_count)
    valset = value_rows.reshape(seq_count * row_count, feat_count)
    state_terms = state_terms_of(keyset, valset, 8)
    prefix_bf = pair_chain_prefix(state_terms, "ctx", 8)
    normed = attend_of(query, keyset, valset, prefix_bf, full_gain, 8)
    return normed.reshape(seq_count, row_count, feat_count)


def solution(mesh):
    in_specs = (
        P(("groups", "dp"), "ctx", None),
        P(("groups", "dp"), "ctx", None),
        P(("groups", "dp"), "ctx", None),
        P("dp"),
    )
    out_specs = P(("groups", "dp"), "ctx", None)
    return jax.shard_map(shards, mesh=mesh, in_specs=in_specs, out_specs=out_specs, check_vma=False)
```

```python
import jax
import jax.numpy as jnp
from jax import lax
from jax.experimental import pallas as pl
from jax.experimental.pallas import tpu as pltpu
from jax.sharding import PartitionSpec as P

H = 32


def pair_chain_prefix(terms, pieces):
    levels = lax.axis_size("ctx_hi")
    mine_at = lax.axis_index("ctx_lo")
    first = mine_at == 0
    half = terms.shape[0] // 2
    mine_all = lax.dynamic_slice_in_dim(terms, mine_at * half, half, 0)
    total_all = lax.psum_scatter(terms, "ctx_lo", scatter_dimension=0, tiled=True)
    step = half // pieces
    keeps, sends = [], []
    for piece in range(pieces):
        mine = mine_all[piece * step:(piece + 1) * step]
        total = total_all[piece * step:(piece + 1) * step]
        carried = jnp.zeros_like(total)
        for hop in range(1, levels):
            carried = carried + lax.ppermute(carried + total, "ctx_hi", [(hop - 1, hop)])
        keeps.append((carried + jnp.where(first, 0.0, total - mine)).astype(jnp.bfloat16))
        sends.append((carried + jnp.where(first, mine, 0.0)).astype(jnp.bfloat16))
    keep = jnp.concatenate(keeps, axis=0)
    both = lax.all_gather(jnp.concatenate(sends, axis=0), "ctx_lo", axis=0, tiled=False)
    back = lax.dynamic_index_in_dim(both, 1 - mine_at, 0, keepdims=False)
    low = jnp.where(first, keep, back)
    high = jnp.where(first, back, keep)
    return jnp.concatenate([low, high], axis=0)


def state_kernel(key_ref, val_ref, out_ref):
    heads, head_size, _ = out_ref.shape
    for head in range(heads):
        cols = slice(head * head_size, (head + 1) * head_size)
        out_ref[head] = lax.dot_general(
            key_ref[:, cols], val_ref[:, cols], (((0,), (0,)), ((), ())),
            preferred_element_type=jnp.float32)


def state_terms_of(keyset, valset, group):
    row_count, feat_count = keyset.shape
    head_size = feat_count // H
    width = group * head_size
    return pl.pallas_call(
        state_kernel,
        grid=(H // group,),
        in_specs=[pl.BlockSpec((row_count, width), lambda g: (0, g)),
                  pl.BlockSpec((row_count, width), lambda g: (0, g))],
        out_specs=pl.BlockSpec((group, head_size, head_size), lambda g: (g, 0, 0)),
        out_shape=jax.ShapeDtypeStruct((H, head_size, head_size), jnp.float32),
    )(keyset, valset)


def attend_kernel(query_ref, key_ref, val_ref, prefix_ref, gain_ref, out_ref, acc_ref, sumsq_ref):
    step = pl.program_id(0)
    row_count, width = query_ref.shape
    heads, head_size, _ = prefix_ref.shape
    causal = (lax.broadcasted_iota(jnp.int32, (row_count, row_count), 0)
              >= lax.broadcasted_iota(jnp.int32, (row_count, row_count), 1))

    @pl.when(step == 0)
    def _():
        sumsq_ref[...] = jnp.zeros_like(sumsq_ref)

    sumsq = sumsq_ref[...]
    for head in range(heads):
        cols = slice(head * head_size, (head + 1) * head_size)
        query = query_ref[:, cols]
        scores = lax.dot_general(query, key_ref[:, cols], (((1,), (1,)), ((), ())),
                                 preferred_element_type=jnp.float32)
        weights = jnp.where(causal, scores, 0.0).astype(jnp.bfloat16)
        within = jnp.dot(weights, val_ref[:, cols], preferred_element_type=jnp.float32)
        carried = jnp.dot(query, prefix_ref[head], preferred_element_type=jnp.float32)
        attended = within + carried
        acc_ref[step, :, cols] = attended
        sumsq = sumsq + jnp.sum(attended * attended, axis=1, keepdims=True)
    sumsq_ref[...] = sumsq

    @pl.when(step == pl.num_programs(0) - 1)
    def _():
        scale = lax.rsqrt(sumsq / (width * pl.num_programs(0)) + 1e-05)
        for part in range(acc_ref.shape[0]):
            cols = slice(part * width, (part + 1) * width)
            out_ref[:, cols] = (acc_ref[part] * scale * gain_ref[:, cols]).astype(out_ref.dtype)


def attend_of(query, keyset, valset, prefix_bf, full_gain, group):
    row_count, feat_count = query.shape
    head_size = feat_count // H
    width = group * head_size
    steps = H // group
    return pl.pallas_call(
        attend_kernel,
        grid=(steps,),
        in_specs=[pl.BlockSpec((row_count, width), lambda g: (0, g)),
                  pl.BlockSpec((row_count, width), lambda g: (0, g)),
                  pl.BlockSpec((row_count, width), lambda g: (0, g)),
                  pl.BlockSpec((group, head_size, head_size), lambda g: (g, 0, 0)),
                  pl.BlockSpec((1, feat_count), lambda g: (0, 0))],
        out_specs=pl.BlockSpec((row_count, feat_count), lambda g: (0, 0)),
        out_shape=jax.ShapeDtypeStruct((row_count, feat_count), jnp.bfloat16),
        scratch_shapes=[pltpu.VMEM((steps, row_count, width), jnp.float32),
                        pltpu.VMEM((row_count, 1), jnp.float32)],
    )(query, keyset, valset, prefix_bf, full_gain)


def shards(query_rows, key_rows, value_rows, gain):
    seq_count, row_count, feat_count = query_rows.shape
    full_gain = lax.all_gather(gain, "dp", axis=0, tiled=True).reshape(1, feat_count)
    query = query_rows.reshape(seq_count * row_count, feat_count)
    keyset = key_rows.reshape(seq_count * row_count, feat_count)
    valset = value_rows.reshape(seq_count * row_count, feat_count)
    state_terms = state_terms_of(keyset, valset, 8)
    prefix_bf = pair_chain_prefix(state_terms, 4)
    normed = attend_of(query, keyset, valset, prefix_bf, full_gain, 8)
    return normed.reshape(seq_count, row_count, feat_count)


def solution(mesh):
    devices = mesh.devices
    sizes = dict(zip(mesh.axis_names, devices.shape))
    ctx_at = mesh.axis_names.index("ctx")
    split = devices.shape[:ctx_at] + (sizes["ctx"] // 2, 2) + devices.shape[ctx_at + 1:]
    names = mesh.axis_names[:ctx_at] + ("ctx_hi", "ctx_lo") + mesh.axis_names[ctx_at + 1:]
    paired = jax.sharding.Mesh(devices.reshape(split), names)
    rows = P(("groups", "dp"), ("ctx_hi", "ctx_lo"), None)
    in_specs = (rows, rows, rows, P("dp"))
    return jax.shard_map(shards, mesh=paired, in_specs=in_specs, out_specs=rows, check_vma=False)
```

```python
import jax
import jax.numpy as jnp
from jax import lax
from jax.experimental import pallas as pl
from jax.experimental.pallas import tpu as pltpu
from jax.sharding import PartitionSpec as P

H = 32


def pair_chain_prefix(terms, axis, pieces):
    count = lax.axis_size(axis)
    mine_at = lax.axis_index(axis) % 2
    first = mine_at == 0
    half = terms.shape[0] // 2
    pairs = count // 2
    mine_all = lax.dynamic_slice_in_dim(terms, mine_at * half, half, 0)
    other_all = lax.dynamic_slice_in_dim(terms, (1 - mine_at) * half, half, 0)
    swap = [(2 * i, 2 * i + 1) for i in range(pairs)] + [(2 * i + 1, 2 * i) for i in range(pairs)]
    step = half // pieces
    keeps, backs = [], []
    for piece in range(pieces):
        mine = mine_all[piece * step:(piece + 1) * step]
        got = lax.ppermute(other_all[piece * step:(piece + 1) * step], axis, swap)
        total = mine + got
        carried = jnp.zeros_like(total)
        for hop in range(1, pairs):
            links = [(2 * (hop - 1) + side, 2 * hop + side) for side in range(2)]
            carried = carried + lax.ppermute(carried + total, axis, links)
        keeps.append((carried + jnp.where(first, 0.0, got)).astype(jnp.bfloat16))
        send = (carried + jnp.where(first, mine, 0.0)).astype(jnp.bfloat16)
        backs.append(lax.ppermute(send, axis, swap))
    keep = jnp.concatenate(keeps, axis=0)
    back = jnp.concatenate(backs, axis=0)
    low = jnp.where(first, keep, back)
    high = jnp.where(first, back, keep)
    return jnp.concatenate([low, high], axis=0)


def state_kernel(key_ref, val_ref, out_ref):
    heads, head_size, _ = out_ref.shape
    for head in range(heads):
        cols = slice(head * head_size, (head + 1) * head_size)
        out_ref[head] = lax.dot_general(
            key_ref[:, cols], val_ref[:, cols], (((0,), (0,)), ((), ())),
            preferred_element_type=jnp.float32)


def state_terms_of(keyset, valset, group):
    row_count, feat_count = keyset.shape
    head_size = feat_count // H
    width = group * head_size
    return pl.pallas_call(
        state_kernel,
        grid=(H // group,),
        in_specs=[pl.BlockSpec((row_count, width), lambda g: (0, g)),
                  pl.BlockSpec((row_count, width), lambda g: (0, g))],
        out_specs=pl.BlockSpec((group, head_size, head_size), lambda g: (g, 0, 0)),
        out_shape=jax.ShapeDtypeStruct((H, head_size, head_size), jnp.float32),
    )(keyset, valset)


def attend_kernel(query_ref, key_ref, val_ref, prefix_ref, gain_ref, out_ref, acc_ref, sumsq_ref):
    step = pl.program_id(0)
    row_count, width = query_ref.shape
    heads, head_size, _ = prefix_ref.shape
    causal = (lax.broadcasted_iota(jnp.int32, (row_count, row_count), 0)
              >= lax.broadcasted_iota(jnp.int32, (row_count, row_count), 1))

    @pl.when(step == 0)
    def _():
        sumsq_ref[...] = jnp.zeros_like(sumsq_ref)

    sumsq = sumsq_ref[...]
    for head in range(heads):
        cols = slice(head * head_size, (head + 1) * head_size)
        query = query_ref[:, cols]
        scores = lax.dot_general(query, key_ref[:, cols], (((1,), (1,)), ((), ())),
                                 preferred_element_type=jnp.float32)
        weights = jnp.where(causal, scores, 0.0).astype(jnp.bfloat16)
        lhs = jnp.concatenate([weights, query], axis=1)
        rhs = jnp.concatenate([val_ref[:, cols], prefix_ref[head]], axis=0)
        attended = jnp.dot(lhs, rhs, preferred_element_type=jnp.float32)
        acc_ref[step, :, cols] = attended
        sumsq = sumsq + attended * attended
    sumsq_ref[...] = sumsq

    @pl.when(step == pl.num_programs(0) - 1)
    def _():
        total = jnp.sum(sumsq, axis=1, keepdims=True)
        scale = lax.rsqrt(total / (width * pl.num_programs(0)) + 1e-05)
        for part in range(acc_ref.shape[0]):
            cols = slice(part * width, (part + 1) * width)
            out_ref[:, cols] = (acc_ref[part] * scale * gain_ref[:, cols]).astype(out_ref.dtype)


def attend_of(query, keyset, valset, prefix_bf, full_gain, group):
    row_count, feat_count = query.shape
    head_size = feat_count // H
    width = group * head_size
    steps = H // group
    return pl.pallas_call(
        attend_kernel,
        grid=(steps,),
        in_specs=[pl.BlockSpec((row_count, width), lambda g: (0, g)),
                  pl.BlockSpec((row_count, width), lambda g: (0, g)),
                  pl.BlockSpec((row_count, width), lambda g: (0, g)),
                  pl.BlockSpec((group, head_size, head_size), lambda g: (g, 0, 0)),
                  pl.BlockSpec((1, feat_count), lambda g: (0, 0))],
        out_specs=pl.BlockSpec((row_count, feat_count), lambda g: (0, 0)),
        out_shape=jax.ShapeDtypeStruct((row_count, feat_count), jnp.bfloat16),
        scratch_shapes=[pltpu.VMEM((steps, row_count, width), jnp.float32),
                        pltpu.VMEM((row_count, head_size), jnp.float32)],
    )(query, keyset, valset, prefix_bf, full_gain)


def shards(query_rows, key_rows, value_rows, gain):
    seq_count, row_count, feat_count = query_rows.shape
    pair = [(0, 1), (1, 0)] if lax.axis_size("dp") == 2 else None
    if pair is None:
        full_gain = lax.all_gather(gain, "dp", axis=0, tiled=True).reshape(1, feat_count)
    else:
        other_gain = lax.ppermute(gain, "dp", pair)
        low_first = lax.axis_index("dp") == 0
        full_gain = jnp.concatenate([jnp.where(low_first, gain, other_gain),
                                     jnp.where(low_first, other_gain, gain)]).reshape(1, feat_count)
    query = query_rows.reshape(seq_count * row_count, feat_count)
    keyset = key_rows.reshape(seq_count * row_count, feat_count)
    valset = value_rows.reshape(seq_count * row_count, feat_count)
    state_terms = state_terms_of(keyset, valset, 16)
    prefix_bf = pair_chain_prefix(state_terms, "ctx", 4)
    normed = attend_of(query, keyset, valset, prefix_bf, full_gain, 8)
    return normed.reshape(seq_count, row_count, feat_count)


def solution(mesh):
    in_specs = (
        P(("groups", "dp"), "ctx", None),
        P(("groups", "dp"), "ctx", None),
        P(("groups", "dp"), "ctx", None),
        P("dp"),
    )
    out_specs = P(("groups", "dp"), "ctx", None)
    return jax.shard_map(shards, mesh=mesh, in_specs=in_specs, out_specs=out_specs, check_vma=False)
```

```python
import jax
import jax.numpy as jnp
from jax import lax
from jax.experimental import pallas as pl
from jax.experimental.pallas import tpu as pltpu
from jax.sharding import PartitionSpec as P

H = 32


def pair_chain_prefix(terms, axis, pieces):
    count = lax.axis_size(axis)
    mine_at = lax.axis_index(axis) % 2
    first = mine_at == 0
    half = terms.shape[0] // 2
    pairs = count // 2
    mine_all = lax.dynamic_slice_in_dim(terms, mine_at * half, half, 0)
    other_all = lax.dynamic_slice_in_dim(terms, (1 - mine_at) * half, half, 0)
    swap = [(2 * i, 2 * i + 1) for i in range(pairs)] + [(2 * i + 1, 2 * i) for i in range(pairs)]
    step = half // pieces
    keeps, backs = [], []
    for piece in range(pieces):
        mine = mine_all[piece * step:(piece + 1) * step]
        got = lax.ppermute(other_all[piece * step:(piece + 1) * step], axis, swap)
        total = mine + got
        carried = jnp.zeros_like(total)
        for hop in range(1, pairs):
            links = [(2 * (hop - 1) + side, 2 * hop + side) for side in range(2)]
            came = lax.ppermute(carried + total, axis, links)
            if hop == pairs - 1 and backs:
                came, _ = lax.optimization_barrier((came, backs[-1]))
            carried = carried + came
        keeps.append((carried + jnp.where(first, 0.0, got)).astype(jnp.bfloat16))
        send = (carried + jnp.where(first, mine, 0.0)).astype(jnp.bfloat16)
        backs.append(lax.ppermute(send, axis, swap))
    keep = jnp.concatenate(keeps, axis=0)
    back = jnp.concatenate(backs, axis=0)
    low = jnp.where(first, keep, back)
    high = jnp.where(first, back, keep)
    return jnp.concatenate([low, high], axis=0)


def state_kernel(key_ref, val_ref, out_ref):
    heads, head_size, _ = out_ref.shape
    for head in range(heads):
        cols = slice(head * head_size, (head + 1) * head_size)
        out_ref[head] = lax.dot_general(
            key_ref[:, cols], val_ref[:, cols], (((0,), (0,)), ((), ())),
            preferred_element_type=jnp.float32)


def state_terms_of(keyset, valset, group):
    row_count, feat_count = keyset.shape
    head_size = feat_count // H
    width = group * head_size
    return pl.pallas_call(
        state_kernel,
        grid=(H // group,),
        in_specs=[pl.BlockSpec((row_count, width), lambda g: (0, g)),
                  pl.BlockSpec((row_count, width), lambda g: (0, g))],
        out_specs=pl.BlockSpec((group, head_size, head_size), lambda g: (g, 0, 0)),
        out_shape=jax.ShapeDtypeStruct((H, head_size, head_size), jnp.float32),
    )(keyset, valset)


def attend_kernel(query_ref, key_ref, val_ref, prefix_ref, gain_ref, out_ref, acc_ref, sumsq_ref):
    step = pl.program_id(0)
    row_count, width = query_ref.shape
    heads, head_size, _ = prefix_ref.shape
    causal = (lax.broadcasted_iota(jnp.int32, (row_count, row_count), 0)
              >= lax.broadcasted_iota(jnp.int32, (row_count, row_count), 1))

    @pl.when(step == 0)
    def _():
        sumsq_ref[...] = jnp.zeros_like(sumsq_ref)

    sumsq = sumsq_ref[...]
    for head in range(heads):
        cols = slice(head * head_size, (head + 1) * head_size)
        query = query_ref[:, cols]
        scores = lax.dot_general(query, key_ref[:, cols], (((1,), (1,)), ((), ())),
                                 preferred_element_type=jnp.float32)
        weights = jnp.where(causal, scores, 0.0).astype(jnp.bfloat16)
        lhs = jnp.concatenate([weights, query], axis=1)
        rhs = jnp.concatenate([val_ref[:, cols], prefix_ref[head]], axis=0)
        attended = jnp.dot(lhs, rhs, preferred_element_type=jnp.float32)
        acc_ref[step, :, cols] = attended
        sumsq = sumsq + attended * attended
    sumsq_ref[...] = sumsq

    @pl.when(step == pl.num_programs(0) - 1)
    def _():
        total = jnp.sum(sumsq, axis=1, keepdims=True)
        scale = lax.rsqrt(total / (width * pl.num_programs(0)) + 1e-05)
        for part in range(acc_ref.shape[0]):
            cols = slice(part * width, (part + 1) * width)
            out_ref[:, cols] = (acc_ref[part] * scale * gain_ref[:, cols]).astype(out_ref.dtype)


def attend_of(query, keyset, valset, prefix_bf, full_gain, group):
    row_count, feat_count = query.shape
    head_size = feat_count // H
    width = group * head_size
    steps = H // group
    return pl.pallas_call(
        attend_kernel,
        grid=(steps,),
        in_specs=[pl.BlockSpec((row_count, width), lambda g: (0, g)),
                  pl.BlockSpec((row_count, width), lambda g: (0, g)),
                  pl.BlockSpec((row_count, width), lambda g: (0, g)),
                  pl.BlockSpec((group, head_size, head_size), lambda g: (g, 0, 0)),
                  pl.BlockSpec((1, feat_count), lambda g: (0, 0))],
        out_specs=pl.BlockSpec((row_count, feat_count), lambda g: (0, 0)),
        out_shape=jax.ShapeDtypeStruct((row_count, feat_count), jnp.bfloat16),
        scratch_shapes=[pltpu.VMEM((steps, row_count, width), jnp.float32),
                        pltpu.VMEM((row_count, head_size), jnp.float32)],
    )(query, keyset, valset, prefix_bf, full_gain)


def shards(query_rows, key_rows, value_rows, gain):
    seq_count, row_count, feat_count = query_rows.shape
    pair = [(0, 1), (1, 0)] if lax.axis_size("dp") == 2 else None
    if pair is None:
        full_gain = lax.all_gather(gain, "dp", axis=0, tiled=True).reshape(1, feat_count)
    else:
        other_gain = lax.ppermute(gain, "dp", pair)
        low_first = lax.axis_index("dp") == 0
        full_gain = jnp.concatenate([jnp.where(low_first, gain, other_gain),
                                     jnp.where(low_first, other_gain, gain)]).reshape(1, feat_count)
    query = query_rows.reshape(seq_count * row_count, feat_count)
    keyset = key_rows.reshape(seq_count * row_count, feat_count)
    valset = value_rows.reshape(seq_count * row_count, feat_count)
    state_terms = state_terms_of(keyset, valset, 16)
    prefix_bf = pair_chain_prefix(state_terms, "ctx", 4)
    normed = attend_of(query, keyset, valset, prefix_bf, full_gain, 8)
    return normed.reshape(seq_count, row_count, feat_count)


def solution(mesh):
    in_specs = (
        P(("groups", "dp"), "ctx", None),
        P(("groups", "dp"), "ctx", None),
        P(("groups", "dp"), "ctx", None),
        P("dp"),
    )
    out_specs = P(("groups", "dp"), "ctx", None)
    return jax.shard_map(shards, mesh=mesh, in_specs=in_specs, out_specs=out_specs, check_vma=False)
```

```python
import jax
import jax.numpy as jnp
from jax import lax
from jax.experimental import pallas as pl
from jax.experimental.pallas import tpu as pltpu
from jax.sharding import PartitionSpec as P

H = 32


def pair_chain_prefix(terms, axis, pieces):
    count = lax.axis_size(axis)
    mine_at = lax.axis_index(axis) % 2
    first = mine_at == 0
    half = terms.shape[0] // 2
    pairs = count // 2
    mine_all = lax.dynamic_slice_in_dim(terms, mine_at * half, half, 0)
    other_all = lax.dynamic_slice_in_dim(terms, (1 - mine_at) * half, half, 0)
    swap = [(2 * i, 2 * i + 1) for i in range(pairs)] + [(2 * i + 1, 2 * i) for i in range(pairs)]
    got_all = lax.ppermute(other_all, axis, swap)
    step = half // pieces
    keeps, backs = [], []
    for piece in range(pieces):
        mine = mine_all[piece * step:(piece + 1) * step]
        got = got_all[piece * step:(piece + 1) * step]
        total = mine + got
        carried = jnp.zeros_like(total)
        for hop in range(1, pairs):
            links = [(2 * (hop - 1) + side, 2 * hop + side) for side in range(2)]
            carried = carried + lax.ppermute(carried + total, axis, links)
        keeps.append((carried + jnp.where(first, 0.0, got)).astype(jnp.bfloat16))
        send = (carried + jnp.where(first, mine, 0.0)).astype(jnp.bfloat16)
        backs.append(lax.ppermute(send, axis, swap))
    keep = jnp.concatenate(keeps, axis=0)
    back = jnp.concatenate(backs, axis=0)
    low = jnp.where(first, keep, back)
    high = jnp.where(first, back, keep)
    return jnp.concatenate([low, high], axis=0)


def state_kernel(key_ref, val_ref, out_ref):
    heads, head_size, _ = out_ref.shape
    for head in range(heads):
        cols = slice(head * head_size, (head + 1) * head_size)
        out_ref[head] = lax.dot_general(
            key_ref[:, cols], val_ref[:, cols], (((0,), (0,)), ((), ())),
            preferred_element_type=jnp.float32)


def state_terms_of(keyset, valset, group):
    row_count, feat_count = keyset.shape
    head_size = feat_count // H
    width = group * head_size
    return pl.pallas_call(
        state_kernel,
        grid=(H // group,),
        in_specs=[pl.BlockSpec((row_count, width), lambda g: (0, g)),
                  pl.BlockSpec((row_count, width), lambda g: (0, g))],
        out_specs=pl.BlockSpec((group, head_size, head_size), lambda g: (g, 0, 0)),
        out_shape=jax.ShapeDtypeStruct((H, head_size, head_size), jnp.float32),
    )(keyset, valset)


def attend_kernel(query_ref, key_ref, val_ref, prefix_ref, gain_ref, out_ref, acc_ref, sumsq_ref):
    step = pl.program_id(0)
    row_count, width = query_ref.shape
    heads, head_size, _ = prefix_ref.shape
    causal = (lax.broadcasted_iota(jnp.int32, (row_count, row_count), 0)
              >= lax.broadcasted_iota(jnp.int32, (row_count, row_count), 1))

    @pl.when(step == 0)
    def _():
        sumsq_ref[...] = jnp.zeros_like(sumsq_ref)

    sumsq = sumsq_ref[...]
    for head in range(heads):
        cols = slice(head * head_size, (head + 1) * head_size)
        query = query_ref[:, cols]
        scores = lax.dot_general(query, key_ref[:, cols], (((1,), (1,)), ((), ())),
                                 preferred_element_type=jnp.float32)
        weights = jnp.where(causal, scores, 0.0).astype(jnp.bfloat16)
        lhs = jnp.concatenate([weights, query], axis=1)
        rhs = jnp.concatenate([val_ref[:, cols], prefix_ref[head]], axis=0)
        attended = jnp.dot(lhs, rhs, preferred_element_type=jnp.float32)
        acc_ref[step, :, cols] = attended
        sumsq = sumsq + attended * attended
    sumsq_ref[...] = sumsq

    @pl.when(step == pl.num_programs(0) - 1)
    def _():
        total = jnp.sum(sumsq, axis=1, keepdims=True)
        scale = lax.rsqrt(total / (width * pl.num_programs(0)) + 1e-05)
        for part in range(acc_ref.shape[0]):
            cols = slice(part * width, (part + 1) * width)
            out_ref[:, cols] = (acc_ref[part] * scale * gain_ref[:, cols]).astype(out_ref.dtype)


def attend_of(query, keyset, valset, prefix_bf, full_gain, group):
    row_count, feat_count = query.shape
    head_size = feat_count // H
    width = group * head_size
    steps = H // group
    return pl.pallas_call(
        attend_kernel,
        grid=(steps,),
        in_specs=[pl.BlockSpec((row_count, width), lambda g: (0, g)),
                  pl.BlockSpec((row_count, width), lambda g: (0, g)),
                  pl.BlockSpec((row_count, width), lambda g: (0, g)),
                  pl.BlockSpec((group, head_size, head_size), lambda g: (g, 0, 0)),
                  pl.BlockSpec((1, feat_count), lambda g: (0, 0))],
        out_specs=pl.BlockSpec((row_count, feat_count), lambda g: (0, 0)),
        out_shape=jax.ShapeDtypeStruct((row_count, feat_count), jnp.bfloat16),
        scratch_shapes=[pltpu.VMEM((steps, row_count, width), jnp.float32),
                        pltpu.VMEM((row_count, head_size), jnp.float32)],
    )(query, keyset, valset, prefix_bf, full_gain)


def shards(query_rows, key_rows, value_rows, gain):
    seq_count, row_count, feat_count = query_rows.shape
    pair = [(0, 1), (1, 0)] if lax.axis_size("dp") == 2 else None
    if pair is None:
        full_gain = lax.all_gather(gain, "dp", axis=0, tiled=True).reshape(1, feat_count)
    else:
        other_gain = lax.ppermute(gain, "dp", pair)
        low_first = lax.axis_index("dp") == 0
        full_gain = jnp.concatenate([jnp.where(low_first, gain, other_gain),
                                     jnp.where(low_first, other_gain, gain)]).reshape(1, feat_count)
    query = query_rows.reshape(seq_count * row_count, feat_count)
    keyset = key_rows.reshape(seq_count * row_count, feat_count)
    valset = value_rows.reshape(seq_count * row_count, feat_count)
    state_terms = state_terms_of(keyset, valset, 16)
    prefix_bf = pair_chain_prefix(state_terms, "ctx", 4)
    normed = attend_of(query, keyset, valset, prefix_bf, full_gain, 8)
    return normed.reshape(seq_count, row_count, feat_count)


def solution(mesh):
    in_specs = (
        P(("groups", "dp"), "ctx", None),
        P(("groups", "dp"), "ctx", None),
        P(("groups", "dp"), "ctx", None),
        P("dp"),
    )
    out_specs = P(("groups", "dp"), "ctx", None)
    return jax.shard_map(shards, mesh=mesh, in_specs=in_specs, out_specs=out_specs, check_vma=False)
```

```python
import jax
import jax.numpy as jnp
from jax import lax
from jax.experimental import pallas as pl
from jax.experimental.pallas import tpu as pltpu
from jax.sharding import PartitionSpec as P

H = 32


def pair_chain_prefix(terms, axis, pieces):
    count = lax.axis_size(axis)
    mine_at = lax.axis_index(axis) % 2
    first = mine_at == 0
    half = terms.shape[0] // 2
    pairs = count // 2
    mine_all = lax.dynamic_slice_in_dim(terms, mine_at * half, half, 0)
    other_all = lax.dynamic_slice_in_dim(terms, (1 - mine_at) * half, half, 0)
    swap = [(2 * i, 2 * i + 1) for i in range(pairs)] + [(2 * i + 1, 2 * i) for i in range(pairs)]
    step = half // pieces
    keeps, backs = [], []
    got, came = None, [None] * pairs
    for piece in range(pieces):
        mine = mine_all[piece * step:(piece + 1) * step]
        other = other_all[piece * step:(piece + 1) * step]
        if got is not None:
            other, _ = lax.optimization_barrier((other, got))
        got = lax.ppermute(other, axis, swap)
        total = mine + got
        carried = jnp.zeros_like(total)
        for hop in range(1, pairs):
            links = [(2 * (hop - 1) + side, 2 * hop + side) for side in range(2)]
            send = carried + total
            if came[hop] is not None:
                send, _ = lax.optimization_barrier((send, came[hop]))
            came[hop] = lax.ppermute(send, axis, links)
            carried = carried + came[hop]
        keeps.append((carried + jnp.where(first, 0.0, got)).astype(jnp.bfloat16))
        send = (carried + jnp.where(first, mine, 0.0)).astype(jnp.bfloat16)
        backs.append(lax.ppermute(send, axis, swap))
    keep = jnp.concatenate(keeps, axis=0)
    back = jnp.concatenate(backs, axis=0)
    low = jnp.where(first, keep, back)
    high = jnp.where(first, back, keep)
    return jnp.concatenate([low, high], axis=0)


def state_kernel(key_ref, val_ref, out_ref):
    heads, head_size, _ = out_ref.shape
    for head in range(heads):
        cols = slice(head * head_size, (head + 1) * head_size)
        out_ref[head] = lax.dot_general(
            key_ref[:, cols], val_ref[:, cols], (((0,), (0,)), ((), ())),
            preferred_element_type=jnp.float32)


def state_terms_of(keyset, valset, group):
    row_count, feat_count = keyset.shape
    head_size = feat_count // H
    width = group * head_size
    return pl.pallas_call(
        state_kernel,
        grid=(H // group,),
        in_specs=[pl.BlockSpec((row_count, width), lambda g: (0, g)),
                  pl.BlockSpec((row_count, width), lambda g: (0, g))],
        out_specs=pl.BlockSpec((group, head_size, head_size), lambda g: (g, 0, 0)),
        out_shape=jax.ShapeDtypeStruct((H, head_size, head_size), jnp.float32),
    )(keyset, valset)


def attend_kernel(query_ref, key_ref, val_ref, prefix_ref, gain_ref, out_ref, acc_ref, sumsq_ref):
    step = pl.program_id(0)
    row_count, width = query_ref.shape
    heads, head_size, _ = prefix_ref.shape
    causal = (lax.broadcasted_iota(jnp.int32, (row_count, row_count), 0)
              >= lax.broadcasted_iota(jnp.int32, (row_count, row_count), 1))

    @pl.when(step == 0)
    def _():
        sumsq_ref[...] = jnp.zeros_like(sumsq_ref)

    sumsq = sumsq_ref[...]
    for head in range(heads):
        cols = slice(head * head_size, (head + 1) * head_size)
        query = query_ref[:, cols]
        scores = lax.dot_general(query, key_ref[:, cols], (((1,), (1,)), ((), ())),
                                 preferred_element_type=jnp.float32)
        weights = jnp.where(causal, scores, 0.0).astype(jnp.bfloat16)
        lhs = jnp.concatenate([weights, query], axis=1)
        rhs = jnp.concatenate([val_ref[:, cols], prefix_ref[head]], axis=0)
        attended = jnp.dot(lhs, rhs, preferred_element_type=jnp.float32)
        acc_ref[step, :, cols] = attended
        sumsq = sumsq + attended * attended
    sumsq_ref[...] = sumsq

    @pl.when(step == pl.num_programs(0) - 1)
    def _():
        total = jnp.sum(sumsq, axis=1, keepdims=True)
        scale = lax.rsqrt(total / (width * pl.num_programs(0)) + 1e-05)
        for part in range(acc_ref.shape[0]):
            cols = slice(part * width, (part + 1) * width)
            out_ref[:, cols] = (acc_ref[part] * scale * gain_ref[:, cols]).astype(out_ref.dtype)


def attend_of(query, keyset, valset, prefix_bf, full_gain, group):
    row_count, feat_count = query.shape
    head_size = feat_count // H
    width = group * head_size
    steps = H // group
    return pl.pallas_call(
        attend_kernel,
        grid=(steps,),
        in_specs=[pl.BlockSpec((row_count, width), lambda g: (0, g)),
                  pl.BlockSpec((row_count, width), lambda g: (0, g)),
                  pl.BlockSpec((row_count, width), lambda g: (0, g)),
                  pl.BlockSpec((group, head_size, head_size), lambda g: (g, 0, 0)),
                  pl.BlockSpec((1, feat_count), lambda g: (0, 0))],
        out_specs=pl.BlockSpec((row_count, feat_count), lambda g: (0, 0)),
        out_shape=jax.ShapeDtypeStruct((row_count, feat_count), jnp.bfloat16),
        scratch_shapes=[pltpu.VMEM((steps, row_count, width), jnp.float32),
                        pltpu.VMEM((row_count, head_size), jnp.float32)],
    )(query, keyset, valset, prefix_bf, full_gain)


def shards(query_rows, key_rows, value_rows, gain):
    seq_count, row_count, feat_count = query_rows.shape
    pair = [(0, 1), (1, 0)] if lax.axis_size("dp") == 2 else None
    if pair is None:
        full_gain = lax.all_gather(gain, "dp", axis=0, tiled=True).reshape(1, feat_count)
    else:
        other_gain = lax.ppermute(gain, "dp", pair)
        low_first = lax.axis_index("dp") == 0
        full_gain = jnp.concatenate([jnp.where(low_first, gain, other_gain),
                                     jnp.where(low_first, other_gain, gain)]).reshape(1, feat_count)
    query = query_rows.reshape(seq_count * row_count, feat_count)
    keyset = key_rows.reshape(seq_count * row_count, feat_count)
    valset = value_rows.reshape(seq_count * row_count, feat_count)
    state_terms = state_terms_of(keyset, valset, 16)
    prefix_bf = pair_chain_prefix(state_terms, "ctx", 4)
    normed = attend_of(query, keyset, valset, prefix_bf, full_gain, 8)
    return normed.reshape(seq_count, row_count, feat_count)


def solution(mesh):
    in_specs = (
        P(("groups", "dp"), "ctx", None),
        P(("groups", "dp"), "ctx", None),
        P(("groups", "dp"), "ctx", None),
        P("dp"),
    )
    out_specs = P(("groups", "dp"), "ctx", None)
    return jax.shard_map(shards, mesh=mesh, in_specs=in_specs, out_specs=out_specs, check_vma=False)
```

```python
import jax
import jax.numpy as jnp
from jax import lax
from jax.experimental import pallas as pl
from jax.experimental.pallas import tpu as pltpu
from jax.sharding import PartitionSpec as P

H = 32


def pair_chain_prefix(terms, axis, pieces):
    count = lax.axis_size(axis)
    mine_at = lax.axis_index(axis) % 2
    first = mine_at == 0
    half = terms.shape[0] // 2
    pairs = count // 2
    mine_all = lax.dynamic_slice_in_dim(terms, mine_at * half, half, 0)
    other_all = lax.dynamic_slice_in_dim(terms, (1 - mine_at) * half, half, 0)
    swap = [(2 * i, 2 * i + 1) for i in range(pairs)] + [(2 * i + 1, 2 * i) for i in range(pairs)]
    step = half // pieces
    keeps, backs = [], []
    for piece in range(pieces):
        mine = mine_all[piece * step:(piece + 1) * step]
        got = lax.ppermute(other_all[piece * step:(piece + 1) * step], axis, swap)
        total = mine + got
        carried = jnp.zeros_like(total)
        for hop in range(1, pairs):
            links = [(2 * (hop - 1) + side, 2 * hop + side) for side in range(2)]
            carried = carried + lax.ppermute(carried + total, axis, links)
        keeps.append((carried + jnp.where(first, 0.0, got)).astype(jnp.bfloat16))
        send = (carried + jnp.where(first, mine, 0.0)).astype(jnp.bfloat16)
        backs.append(lax.ppermute(send, axis, swap))
    keep = jnp.concatenate(keeps, axis=0)
    back = jnp.concatenate(backs, axis=0)
    low = jnp.where(first, keep, back)
    high = jnp.where(first, back, keep)
    return jnp.concatenate([low, high], axis=0)


def state_kernel(key_ref, val_ref, out_ref):
    heads, head_size, _ = out_ref.shape
    for head in range(heads):
        cols = slice(head * head_size, (head + 1) * head_size)
        out_ref[head] = lax.dot_general(
            key_ref[:, cols], val_ref[:, cols], (((0,), (0,)), ((), ())),
            preferred_element_type=jnp.float32)


def state_terms_of(keyset, valset, group):
    row_count, feat_count = keyset.shape
    head_size = feat_count // H
    width = group * head_size
    return pl.pallas_call(
        state_kernel,
        grid=(H // group,),
        in_specs=[pl.BlockSpec((row_count, width), lambda g: (0, g)),
                  pl.BlockSpec((row_count, width), lambda g: (0, g))],
        out_specs=pl.BlockSpec((group, head_size, head_size), lambda g: (g, 0, 0)),
        out_shape=jax.ShapeDtypeStruct((H, head_size, head_size), jnp.float32),
    )(keyset, valset)


def attend_kernel(query_ref, key_ref, val_ref, prefix_ref, gain_ref, out_ref, acc_ref, sumsq_ref):
    step = pl.program_id(0)
    row_count, width = query_ref.shape
    heads, head_size, _ = prefix_ref.shape
    causal = (lax.broadcasted_iota(jnp.int32, (row_count, row_count), 0)
              >= lax.broadcasted_iota(jnp.int32, (row_count, row_count), 1))

    @pl.when(step == 0)
    def _():
        sumsq_ref[...] = jnp.zeros_like(sumsq_ref)

    sumsq = sumsq_ref[...]
    for head in range(heads):
        cols = slice(head * head_size, (head + 1) * head_size)
        query = query_ref[:, cols]
        scores = lax.dot_general(query, key_ref[:, cols], (((1,), (1,)), ((), ())),
                                 preferred_element_type=jnp.float32)
        weights = jnp.where(causal, scores, 0.0).astype(jnp.bfloat16)
        lhs = jnp.concatenate([weights, query], axis=1)
        rhs = jnp.concatenate([val_ref[:, cols], prefix_ref[head]], axis=0)
        attended = jnp.dot(lhs, rhs, preferred_element_type=jnp.float32)
        acc_ref[step, :, cols] = attended
        sumsq = sumsq + attended * attended
    sumsq_ref[...] = sumsq

    @pl.when(step == pl.num_programs(0) - 1)
    def _():
        total = jnp.sum(sumsq, axis=1, keepdims=True)
        scale = lax.rsqrt(total / (width * pl.num_programs(0)) + 1e-05)
        for part in range(acc_ref.shape[0]):
            cols = slice(part * width, (part + 1) * width)
            out_ref[:, cols] = (acc_ref[part] * scale * gain_ref[:, cols]).astype(out_ref.dtype)


def attend_of(query, keyset, valset, prefix_bf, full_gain, group):
    row_count, feat_count = query.shape
    head_size = feat_count // H
    width = group * head_size
    steps = H // group
    return pl.pallas_call(
        attend_kernel,
        grid=(steps,),
        in_specs=[pl.BlockSpec((row_count, width), lambda g: (0, g)),
                  pl.BlockSpec((row_count, width), lambda g: (0, g)),
                  pl.BlockSpec((row_count, width), lambda g: (0, g)),
                  pl.BlockSpec((group, head_size, head_size), lambda g: (g, 0, 0)),
                  pl.BlockSpec((1, feat_count), lambda g: (0, 0))],
        out_specs=pl.BlockSpec((row_count, feat_count), lambda g: (0, 0)),
        out_shape=jax.ShapeDtypeStruct((row_count, feat_count), jnp.bfloat16),
        scratch_shapes=[pltpu.VMEM((steps, row_count, width), jnp.float32),
                        pltpu.VMEM((row_count, head_size), jnp.float32)],
    )(query, keyset, valset, prefix_bf, full_gain)


def shards(query_rows, key_rows, value_rows, gain):
    seq_count, row_count, feat_count = query_rows.shape
    pair = [(0, 1), (1, 0)] if lax.axis_size("dp") == 2 else None
    if pair is None:
        full_gain = lax.all_gather(gain, "dp", axis=0, tiled=True).reshape(1, feat_count)
    else:
        other_gain = lax.ppermute(gain, "dp", pair)
        low_first = lax.axis_index("dp") == 0
        full_gain = jnp.concatenate([jnp.where(low_first, gain, other_gain),
                                     jnp.where(low_first, other_gain, gain)]).reshape(1, feat_count)
    query = query_rows.reshape(seq_count * row_count, feat_count)
    keyset = key_rows.reshape(seq_count * row_count, feat_count)
    valset = value_rows.reshape(seq_count * row_count, feat_count)
    state_terms = state_terms_of(keyset, valset, 16)
    prefix_bf = pair_chain_prefix(state_terms, "ctx", 2)
    normed = attend_of(query, keyset, valset, prefix_bf, full_gain, 8)
    return normed.reshape(seq_count, row_count, feat_count)


def solution(mesh):
    in_specs = (
        P(("groups", "dp"), "ctx", None),
        P(("groups", "dp"), "ctx", None),
        P(("groups", "dp"), "ctx", None),
        P("dp"),
    )
    out_specs = P(("groups", "dp"), "ctx", None)
    return jax.shard_map(shards, mesh=mesh, in_specs=in_specs, out_specs=out_specs, check_vma=False)
```

```python
import jax
import jax.numpy as jnp
from jax import lax
from jax.experimental import pallas as pl
from jax.experimental.pallas import tpu as pltpu
from jax.sharding import PartitionSpec as P

H = 32


def pair_chain_prefix(terms, axis, pieces):
    count = lax.axis_size(axis)
    mine_at = lax.axis_index(axis) % 2
    first = mine_at == 0
    half = terms.shape[0] // 2
    pairs = count // 2
    mine_all = lax.dynamic_slice_in_dim(terms, mine_at * half, half, 0)
    other_all = lax.dynamic_slice_in_dim(terms, (1 - mine_at) * half, half, 0)
    swap = [(2 * i, 2 * i + 1) for i in range(pairs)] + [(2 * i + 1, 2 * i) for i in range(pairs)]
    step = half // pieces
    keeps, backs = [], []
    for piece in range(pieces):
        mine = mine_all[piece * step:(piece + 1) * step]
        got = lax.ppermute(other_all[piece * step:(piece + 1) * step], axis, swap)
        total = mine + got
        carried = jnp.zeros_like(total)
        for hop in range(1, pairs):
            links = [(2 * (hop - 1) + side, 2 * hop + side) for side in range(2)]
            carried = carried + lax.ppermute(carried + total, axis, links)
        keeps.append((carried + jnp.where(first, 0.0, got)).astype(jnp.bfloat16))
        send = (carried + jnp.where(first, mine, 0.0)).astype(jnp.bfloat16)
        backs.append(lax.ppermute(send, axis, swap))
    return jnp.concatenate(keeps, axis=0), jnp.concatenate(backs, axis=0)


def state_kernel(key_ref, val_ref, out_ref):
    heads, head_size, _ = out_ref.shape
    for head in range(heads):
        cols = slice(head * head_size, (head + 1) * head_size)
        out_ref[head] = lax.dot_general(
            key_ref[:, cols], val_ref[:, cols], (((0,), (0,)), ((), ())),
            preferred_element_type=jnp.float32)


def state_terms_of(keyset, valset, group):
    row_count, feat_count = keyset.shape
    head_size = feat_count // H
    width = group * head_size
    return pl.pallas_call(
        state_kernel,
        grid=(H // group,),
        in_specs=[pl.BlockSpec((row_count, width), lambda g: (0, g)),
                  pl.BlockSpec((row_count, width), lambda g: (0, g))],
        out_specs=pl.BlockSpec((group, head_size, head_size), lambda g: (g, 0, 0)),
        out_shape=jax.ShapeDtypeStruct((H, head_size, head_size), jnp.float32),
    )(keyset, valset)


def attend_kernel(mine_ref, query_ref, key_ref, val_ref, keep_ref, back_ref, gain_ref, out_ref, acc_ref,
                  sumsq_ref):
    step = pl.program_id(0)
    row_count, width = query_ref.shape
    heads, head_size, _ = keep_ref.shape
    own = step // (pl.num_programs(0) // 2) == mine_ref[0]
    causal = (lax.broadcasted_iota(jnp.int32, (row_count, row_count), 0)
              >= lax.broadcasted_iota(jnp.int32, (row_count, row_count), 1))

    @pl.when(step == 0)
    def _():
        sumsq_ref[...] = jnp.zeros_like(sumsq_ref)

    sumsq = sumsq_ref[...]
    for head in range(heads):
        cols = slice(head * head_size, (head + 1) * head_size)
        query = query_ref[:, cols]
        scores = lax.dot_general(query, key_ref[:, cols], (((1,), (1,)), ((), ())),
                                 preferred_element_type=jnp.float32)
        weights = jnp.where(causal, scores, 0.0).astype(jnp.bfloat16)
        lhs = jnp.concatenate([weights, query], axis=1)
        prefix = jnp.where(own, keep_ref[head], back_ref[head])
        rhs = jnp.concatenate([val_ref[:, cols], prefix], axis=0)
        attended = jnp.dot(lhs, rhs, preferred_element_type=jnp.float32)
        acc_ref[step, :, cols] = attended
        sumsq = sumsq + attended * attended
    sumsq_ref[...] = sumsq

    @pl.when(step == pl.num_programs(0) - 1)
    def _():
        total = jnp.sum(sumsq, axis=1, keepdims=True)
        scale = lax.rsqrt(total / (width * pl.num_programs(0)) + 1e-05)
        for part in range(acc_ref.shape[0]):
            cols = slice(part * width, (part + 1) * width)
            out_ref[:, cols] = (acc_ref[part] * scale * gain_ref[:, cols]).astype(out_ref.dtype)


def attend_of(query, keyset, valset, keep, back, mine_at, full_gain, group):
    row_count, feat_count = query.shape
    head_size = feat_count // H
    width = group * head_size
    steps = H // group
    spec = pl.BlockSpec((row_count, width), lambda g, at: (0, g))
    half_spec = pl.BlockSpec((group, head_size, head_size), lambda g, at: (g % (steps // 2), 0, 0))
    return pl.pallas_call(
        attend_kernel,
        grid_spec=pltpu.PrefetchScalarGridSpec(
            num_scalar_prefetch=1,
            grid=(steps,),
            in_specs=[spec, spec, spec, half_spec, half_spec,
                      pl.BlockSpec((1, feat_count), lambda g, at: (0, 0))],
            out_specs=pl.BlockSpec((row_count, feat_count), lambda g, at: (0, 0)),
            scratch_shapes=[pltpu.VMEM((steps, row_count, width), jnp.float32),
                            pltpu.VMEM((row_count, head_size), jnp.float32)]),
        out_shape=jax.ShapeDtypeStruct((row_count, feat_count), jnp.bfloat16),
    )(jnp.reshape(mine_at, (1,)).astype(jnp.int32), query, keyset, valset, keep, back, full_gain)


def shards(query_rows, key_rows, value_rows, gain):
    seq_count, row_count, feat_count = query_rows.shape
    pair = [(0, 1), (1, 0)] if lax.axis_size("dp") == 2 else None
    if pair is None:
        full_gain = lax.all_gather(gain, "dp", axis=0, tiled=True).reshape(1, feat_count)
    else:
        other_gain = lax.ppermute(gain, "dp", pair)
        low_first = lax.axis_index("dp") == 0
        full_gain = jnp.concatenate([jnp.where(low_first, gain, other_gain),
                                     jnp.where(low_first, other_gain, gain)]).reshape(1, feat_count)
    query = query_rows.reshape(seq_count * row_count, feat_count)
    keyset = key_rows.reshape(seq_count * row_count, feat_count)
    valset = value_rows.reshape(seq_count * row_count, feat_count)
    state_terms = state_terms_of(keyset, valset, 16)
    keep, back = pair_chain_prefix(state_terms, "ctx", 4)
    normed = attend_of(query, keyset, valset, keep, back, lax.axis_index("ctx") % 2, full_gain, 8)
    return normed.reshape(seq_count, row_count, feat_count)


def solution(mesh):
    in_specs = (
        P(("groups", "dp"), "ctx", None),
        P(("groups", "dp"), "ctx", None),
        P(("groups", "dp"), "ctx", None),
        P("dp"),
    )
    out_specs = P(("groups", "dp"), "ctx", None)
    return jax.shard_map(shards, mesh=mesh, in_specs=in_specs, out_specs=out_specs, check_vma=False)
```

```python
import jax
import jax.numpy as jnp
from jax import lax
from jax.experimental import pallas as pl
from jax.experimental.pallas import tpu as pltpu
from jax.sharding import PartitionSpec as P

H = 32


def pair_chain_prefix(terms, axis, pieces):
    count = lax.axis_size(axis)
    place = lax.axis_index(axis)
    mine_at = place % 2
    first = mine_at == 0
    last = count // 2 - 1
    at_last = place // 2 == last
    half = terms.shape[0] // 2
    mine_all = lax.dynamic_slice_in_dim(terms, mine_at * half, half, 0)
    other_all = lax.dynamic_slice_in_dim(terms, (1 - mine_at) * half, half, 0)
    swap = [(2 * i, 2 * i + 1) for i in range(last)] + [(2 * i + 1, 2 * i) for i in range(last)]
    behind = 2 * (last - 1)
    kv_back = (lax.ppermute(mine_all, axis, [(2 * last, behind)])
               + lax.ppermute(other_all, axis, [(2 * last, behind + 1)]))
    ahead = [(behind, 2 * last), (behind + 1, 2 * last + 1)]
    across = [(behind, 2 * last + 1), (behind + 1, 2 * last)]
    step = half // pieces
    keeps, backs = [], []
    for piece in range(pieces):
        cut = slice(piece * step, (piece + 1) * step)
        mine = mine_all[cut]
        got = lax.ppermute(other_all[cut], axis, swap)
        total = mine + got
        carried = jnp.zeros_like(total)
        for hop in range(1, last):
            links = [(2 * (hop - 1) + side, 2 * hop + side) for side in range(2)]
            carried = carried + lax.ppermute(carried + total, axis, links)
        keep = (carried + jnp.where(first, 0.0, got)).astype(jnp.bfloat16)
        send = (carried + jnp.where(first, mine, 0.0)).astype(jnp.bfloat16)
        back = lax.ppermute(send, axis, swap)
        reach = carried + total
        added = kv_back[cut]
        straight = lax.ppermute((reach + jnp.where(first, 0.0, added)).astype(jnp.bfloat16), axis, ahead)
        diagonal = lax.ppermute((reach + jnp.where(first, added, 0.0)).astype(jnp.bfloat16), axis, across)
        keeps.append(jnp.where(at_last, straight, keep))
        backs.append(jnp.where(at_last, diagonal, back))
    return jnp.concatenate(keeps, axis=0), jnp.concatenate(backs, axis=0)


def state_kernel(key_ref, val_ref, out_ref):
    heads, head_size, _ = out_ref.shape
    for head in range(heads):
        cols = slice(head * head_size, (head + 1) * head_size)
        out_ref[head] = lax.dot_general(
            key_ref[:, cols], val_ref[:, cols], (((0,), (0,)), ((), ())),
            preferred_element_type=jnp.float32)


def state_terms_of(keyset, valset, group):
    row_count, feat_count = keyset.shape
    head_size = feat_count // H
    width = group * head_size
    return pl.pallas_call(
        state_kernel,
        grid=(H // group,),
        in_specs=[pl.BlockSpec((row_count, width), lambda g: (0, g)),
                  pl.BlockSpec((row_count, width), lambda g: (0, g))],
        out_specs=pl.BlockSpec((group, head_size, head_size), lambda g: (g, 0, 0)),
        out_shape=jax.ShapeDtypeStruct((H, head_size, head_size), jnp.float32),
    )(keyset, valset)


def attend_kernel(mine_ref, query_ref, key_ref, val_ref, keep_ref, back_ref, gain_ref, out_ref, acc_ref,
                  sumsq_ref):
    step = pl.program_id(0)
    row_count, width = query_ref.shape
    heads, head_size, _ = keep_ref.shape
    own = step // (pl.num_programs(0) // 2) == mine_ref[0]
    causal = (lax.broadcasted_iota(jnp.int32, (row_count, row_count), 0)
              >= lax.broadcasted_iota(jnp.int32, (row_count, row_count), 1))

    @pl.when(step == 0)
    def _():
        sumsq_ref[...] = jnp.zeros_like(sumsq_ref)

    sumsq = sumsq_ref[...]
    for head in range(heads):
        cols = slice(head * head_size, (head + 1) * head_size)
        query = query_ref[:, cols]
        scores = lax.dot_general(query, key_ref[:, cols], (((1,), (1,)), ((), ())),
                                 preferred_element_type=jnp.float32)
        weights = jnp.where(causal, scores, 0.0).astype(jnp.bfloat16)
        lhs = jnp.concatenate([weights, query], axis=1)
        prefix = jnp.where(own, keep_ref[head], back_ref[head])
        rhs = jnp.concatenate([val_ref[:, cols], prefix], axis=0)
        attended = jnp.dot(lhs, rhs, preferred_element_type=jnp.float32)
        acc_ref[step, :, cols] = attended
        sumsq = sumsq + attended * attended
    sumsq_ref[...] = sumsq

    @pl.when(step == pl.num_programs(0) - 1)
    def _():
        total = jnp.sum(sumsq, axis=1, keepdims=True)
        scale = lax.rsqrt(total / (width * pl.num_programs(0)) + 1e-05)
        for part in range(acc_ref.shape[0]):
            cols = slice(part * width, (part + 1) * width)
            out_ref[:, cols] = (acc_ref[part] * scale * gain_ref[:, cols]).astype(out_ref.dtype)


def attend_of(query, keyset, valset, keep, back, mine_at, full_gain, group):
    row_count, feat_count = query.shape
    head_size = feat_count // H
    width = group * head_size
    steps = H // group
    spec = pl.BlockSpec((row_count, width), lambda g, at: (0, g))
    half_spec = pl.BlockSpec((group, head_size, head_size), lambda g, at: (g % (steps // 2), 0, 0))
    return pl.pallas_call(
        attend_kernel,
        grid_spec=pltpu.PrefetchScalarGridSpec(
            num_scalar_prefetch=1,
            grid=(steps,),
            in_specs=[spec, spec, spec, half_spec, half_spec,
                      pl.BlockSpec((1, feat_count), lambda g, at: (0, 0))],
            out_specs=pl.BlockSpec((row_count, feat_count), lambda g, at: (0, 0)),
            scratch_shapes=[pltpu.VMEM((steps, row_count, width), jnp.float32),
                            pltpu.VMEM((row_count, head_size), jnp.float32)]),
        out_shape=jax.ShapeDtypeStruct((row_count, feat_count), jnp.bfloat16),
    )(jnp.reshape(mine_at, (1,)).astype(jnp.int32), query, keyset, valset, keep, back, full_gain)


def shards(query_rows, key_rows, value_rows, gain):
    seq_count, row_count, feat_count = query_rows.shape
    pair = [(0, 1), (1, 0)] if lax.axis_size("dp") == 2 else None
    if pair is None:
        full_gain = lax.all_gather(gain, "dp", axis=0, tiled=True).reshape(1, feat_count)
    else:
        other_gain = lax.ppermute(gain, "dp", pair)
        low_first = lax.axis_index("dp") == 0
        full_gain = jnp.concatenate([jnp.where(low_first, gain, other_gain),
                                     jnp.where(low_first, other_gain, gain)]).reshape(1, feat_count)
    query = query_rows.reshape(seq_count * row_count, feat_count)
    keyset = key_rows.reshape(seq_count * row_count, feat_count)
    valset = value_rows.reshape(seq_count * row_count, feat_count)
    state_terms = state_terms_of(keyset, valset, 16)
    keep, back = pair_chain_prefix(state_terms, "ctx", 4)
    normed = attend_of(query, keyset, valset, keep, back, lax.axis_index("ctx") % 2, full_gain, 8)
    return normed.reshape(seq_count, row_count, feat_count)


def solution(mesh):
    in_specs = (
        P(("groups", "dp"), "ctx", None),
        P(("groups", "dp"), "ctx", None),
        P(("groups", "dp"), "ctx", None),
        P("dp"),
    )
    out_specs = P(("groups", "dp"), "ctx", None)
    return jax.shard_map(shards, mesh=mesh, in_specs=in_specs, out_specs=out_specs, check_vma=False)
```

```python
import jax
import jax.numpy as jnp
from jax import lax
from jax.experimental import pallas as pl
from jax.experimental.pallas import tpu as pltpu
from jax.sharding import PartitionSpec as P

H = 32


def pair_chain_prefix(terms, axis, pieces):
    count = lax.axis_size(axis)
    mine_at = lax.axis_index(axis) % 2
    first = mine_at == 0
    half = terms.shape[0] // 2
    pairs = count // 2
    mine_all = lax.dynamic_slice_in_dim(terms, mine_at * half, half, 0)
    other_all = lax.dynamic_slice_in_dim(terms, (1 - mine_at) * half, half, 0)
    swap = [(2 * i, 2 * i + 1) for i in range(pairs)] + [(2 * i + 1, 2 * i) for i in range(pairs)]
    step = half // pieces
    keeps, backs = [], []
    for piece in range(pieces):
        mine = mine_all[piece * step:(piece + 1) * step]
        got = lax.ppermute(other_all[piece * step:(piece + 1) * step], axis, swap)
        total = mine + got
        carried = jnp.zeros_like(total)
        for hop in range(1, pairs):
            links = [(2 * (hop - 1) + side, 2 * hop + side) for side in range(2)]
            carried = carried + lax.ppermute(carried + total, axis, links)
        keeps.append((carried + jnp.where(first, 0.0, got)).astype(jnp.bfloat16))
        backs.append((carried + jnp.where(first, mine, 0.0)).astype(jnp.bfloat16))
    back = lax.ppermute(jnp.concatenate(backs, axis=0), axis, swap)
    return jnp.concatenate(keeps, axis=0), back


def state_kernel(key_ref, val_ref, out_ref):
    heads, head_size, _ = out_ref.shape
    for head in range(heads):
        cols = slice(head * head_size, (head + 1) * head_size)
        out_ref[head] = lax.dot_general(
            key_ref[:, cols], val_ref[:, cols], (((0,), (0,)), ((), ())),
            preferred_element_type=jnp.float32)


def state_terms_of(keyset, valset, group):
    row_count, feat_count = keyset.shape
    head_size = feat_count // H
    width = group * head_size
    return pl.pallas_call(
        state_kernel,
        grid=(H // group,),
        in_specs=[pl.BlockSpec((row_count, width), lambda g: (0, g)),
                  pl.BlockSpec((row_count, width), lambda g: (0, g))],
        out_specs=pl.BlockSpec((group, head_size, head_size), lambda g: (g, 0, 0)),
        out_shape=jax.ShapeDtypeStruct((H, head_size, head_size), jnp.float32),
    )(keyset, valset)


def attend_kernel(mine_ref, query_ref, key_ref, val_ref, keep_ref, back_ref, gain_ref, out_ref, acc_ref,
                  sumsq_ref):
    step = pl.program_id(0)
    row_count, width = query_ref.shape
    heads, head_size, _ = keep_ref.shape
    own = step // (pl.num_programs(0) // 2) == mine_ref[0]
    causal = (lax.broadcasted_iota(jnp.int32, (row_count, row_count), 0)
              >= lax.broadcasted_iota(jnp.int32, (row_count, row_count), 1))

    @pl.when(step == 0)
    def _():
        sumsq_ref[...] = jnp.zeros_like(sumsq_ref)

    sumsq = sumsq_ref[...]
    for head in range(heads):
        cols = slice(head * head_size, (head + 1) * head_size)
        query = query_ref[:, cols]
        scores = lax.dot_general(query, key_ref[:, cols], (((1,), (1,)), ((), ())),
                                 preferred_element_type=jnp.float32)
        weights = jnp.where(causal, scores, 0.0).astype(jnp.bfloat16)
        lhs = jnp.concatenate([weights, query], axis=1)
        prefix = jnp.where(own, keep_ref[head], back_ref[head])
        rhs = jnp.concatenate([val_ref[:, cols], prefix], axis=0)
        attended = jnp.dot(lhs, rhs, preferred_element_type=jnp.float32)
        acc_ref[step, :, cols] = attended
        sumsq = sumsq + attended * attended
    sumsq_ref[...] = sumsq

    @pl.when(step == pl.num_programs(0) - 1)
    def _():
        total = jnp.sum(sumsq, axis=1, keepdims=True)
        scale = lax.rsqrt(total / (width * pl.num_programs(0)) + 1e-05)
        for part in range(acc_ref.shape[0]):
            cols = slice(part * width, (part + 1) * width)
            out_ref[:, cols] = (acc_ref[part] * scale * gain_ref[:, cols]).astype(out_ref.dtype)


def attend_of(query, keyset, valset, keep, back, mine_at, full_gain, group):
    row_count, feat_count = query.shape
    head_size = feat_count // H
    width = group * head_size
    steps = H // group
    spec = pl.BlockSpec((row_count, width), lambda g, at: (0, g))
    half_spec = pl.BlockSpec((group, head_size, head_size), lambda g, at: (g % (steps // 2), 0, 0))
    return pl.pallas_call(
        attend_kernel,
        grid_spec=pltpu.PrefetchScalarGridSpec(
            num_scalar_prefetch=1,
            grid=(steps,),
            in_specs=[spec, spec, spec, half_spec, half_spec,
                      pl.BlockSpec((1, feat_count), lambda g, at: (0, 0))],
            out_specs=pl.BlockSpec((row_count, feat_count), lambda g, at: (0, 0)),
            scratch_shapes=[pltpu.VMEM((steps, row_count, width), jnp.float32),
                            pltpu.VMEM((row_count, head_size), jnp.float32)]),
        out_shape=jax.ShapeDtypeStruct((row_count, feat_count), jnp.bfloat16),
    )(jnp.reshape(mine_at, (1,)).astype(jnp.int32), query, keyset, valset, keep, back, full_gain)


def shards(query_rows, key_rows, value_rows, gain):
    seq_count, row_count, feat_count = query_rows.shape
    pair = [(0, 1), (1, 0)] if lax.axis_size("dp") == 2 else None
    if pair is None:
        full_gain = lax.all_gather(gain, "dp", axis=0, tiled=True).reshape(1, feat_count)
    else:
        other_gain = lax.ppermute(gain, "dp", pair)
        low_first = lax.axis_index("dp") == 0
        full_gain = jnp.concatenate([jnp.where(low_first, gain, other_gain),
                                     jnp.where(low_first, other_gain, gain)]).reshape(1, feat_count)
    query = query_rows.reshape(seq_count * row_count, feat_count)
    keyset = key_rows.reshape(seq_count * row_count, feat_count)
    valset = value_rows.reshape(seq_count * row_count, feat_count)
    state_terms = state_terms_of(keyset, valset, 16)
    keep, back = pair_chain_prefix(state_terms, "ctx", 4)
    normed = attend_of(query, keyset, valset, keep, back, lax.axis_index("ctx") % 2, full_gain, 8)
    return normed.reshape(seq_count, row_count, feat_count)


def solution(mesh):
    in_specs = (
        P(("groups", "dp"), "ctx", None),
        P(("groups", "dp"), "ctx", None),
        P(("groups", "dp"), "ctx", None),
        P("dp"),
    )
    out_specs = P(("groups", "dp"), "ctx", None)
    return jax.shard_map(shards, mesh=mesh, in_specs=in_specs, out_specs=out_specs, check_vma=False)
```

```python
import jax
import jax.numpy as jnp
from jax import lax
from jax.experimental import pallas as pl
from jax.experimental.pallas import tpu as pltpu
from jax.sharding import PartitionSpec as P

H = 32


def pair_chain_prefix(terms, axis, pieces):
    count = lax.axis_size(axis)
    mine_at = lax.axis_index(axis) % 2
    first = mine_at == 0
    half = terms.shape[0] // 2
    pairs = count // 2
    mine_all = lax.dynamic_slice_in_dim(terms, mine_at * half, half, 0)
    other_all = lax.dynamic_slice_in_dim(terms, (1 - mine_at) * half, half, 0)
    swap = [(2 * i, 2 * i + 1) for i in range(pairs)] + [(2 * i + 1, 2 * i) for i in range(pairs)]
    ends = [sum(pieces[:n + 1]) * half // sum(pieces) for n in range(len(pieces))]
    keeps, backs = [], []
    for start, end in zip([0] + ends[:-1], ends):
        mine = mine_all[start:end]
        got = lax.ppermute(other_all[start:end], axis, swap)
        total = mine + got
        carried = jnp.zeros_like(total)
        for hop in range(1, pairs):
            links = [(2 * (hop - 1) + side, 2 * hop + side) for side in range(2)]
            carried = carried + lax.ppermute(carried + total, axis, links)
        keeps.append((carried + jnp.where(first, 0.0, got)).astype(jnp.bfloat16))
        send = (carried + jnp.where(first, mine, 0.0)).astype(jnp.bfloat16)
        backs.append(lax.ppermute(send, axis, swap))
    return jnp.concatenate(keeps, axis=0), jnp.concatenate(backs, axis=0)


def state_kernel(key_ref, val_ref, out_ref):
    heads, head_size, _ = out_ref.shape
    for head in range(heads):
        cols = slice(head * head_size, (head + 1) * head_size)
        out_ref[head] = lax.dot_general(
            key_ref[:, cols], val_ref[:, cols], (((0,), (0,)), ((), ())),
            preferred_element_type=jnp.float32)


def state_terms_of(keyset, valset, group):
    row_count, feat_count = keyset.shape
    head_size = feat_count // H
    width = group * head_size
    return pl.pallas_call(
        state_kernel,
        grid=(H // group,),
        in_specs=[pl.BlockSpec((row_count, width), lambda g: (0, g)),
                  pl.BlockSpec((row_count, width), lambda g: (0, g))],
        out_specs=pl.BlockSpec((group, head_size, head_size), lambda g: (g, 0, 0)),
        out_shape=jax.ShapeDtypeStruct((H, head_size, head_size), jnp.float32),
    )(keyset, valset)


def attend_kernel(mine_ref, query_ref, key_ref, val_ref, keep_ref, back_ref, gain_ref, out_ref, acc_ref,
                  sumsq_ref):
    step = pl.program_id(0)
    row_count, width = query_ref.shape
    heads, head_size, _ = keep_ref.shape
    own = step // (pl.num_programs(0) // 2) == mine_ref[0]
    causal = (lax.broadcasted_iota(jnp.int32, (row_count, row_count), 0)
              >= lax.broadcasted_iota(jnp.int32, (row_count, row_count), 1))

    @pl.when(step == 0)
    def _():
        sumsq_ref[...] = jnp.zeros_like(sumsq_ref)

    sumsq = sumsq_ref[...]
    for head in range(heads):
        cols = slice(head * head_size, (head + 1) * head_size)
        query = query_ref[:, cols]
        scores = lax.dot_general(query, key_ref[:, cols], (((1,), (1,)), ((), ())),
                                 preferred_element_type=jnp.float32)
        weights = jnp.where(causal, scores, 0.0).astype(jnp.bfloat16)
        lhs = jnp.concatenate([weights, query], axis=1)
        prefix = jnp.where(own, keep_ref[head], back_ref[head])
        rhs = jnp.concatenate([val_ref[:, cols], prefix], axis=0)
        attended = jnp.dot(lhs, rhs, preferred_element_type=jnp.float32)
        acc_ref[step, :, cols] = attended
        sumsq = sumsq + attended * attended
    sumsq_ref[...] = sumsq

    @pl.when(step == pl.num_programs(0) - 1)
    def _():
        total = jnp.sum(sumsq, axis=1, keepdims=True)
        scale = lax.rsqrt(total / (width * pl.num_programs(0)) + 1e-05)
        for part in range(acc_ref.shape[0]):
            cols = slice(part * width, (part + 1) * width)
            out_ref[:, cols] = (acc_ref[part] * scale * gain_ref[:, cols]).astype(out_ref.dtype)


def attend_of(query, keyset, valset, keep, back, mine_at, full_gain, group):
    row_count, feat_count = query.shape
    head_size = feat_count // H
    width = group * head_size
    steps = H // group
    spec = pl.BlockSpec((row_count, width), lambda g, at: (0, g))
    half_spec = pl.BlockSpec((group, head_size, head_size), lambda g, at: (g % (steps // 2), 0, 0))
    return pl.pallas_call(
        attend_kernel,
        grid_spec=pltpu.PrefetchScalarGridSpec(
            num_scalar_prefetch=1,
            grid=(steps,),
            in_specs=[spec, spec, spec, half_spec, half_spec,
                      pl.BlockSpec((1, feat_count), lambda g, at: (0, 0))],
            out_specs=pl.BlockSpec((row_count, feat_count), lambda g, at: (0, 0)),
            scratch_shapes=[pltpu.VMEM((steps, row_count, width), jnp.float32),
                            pltpu.VMEM((row_count, head_size), jnp.float32)]),
        out_shape=jax.ShapeDtypeStruct((row_count, feat_count), jnp.bfloat16),
    )(jnp.reshape(mine_at, (1,)).astype(jnp.int32), query, keyset, valset, keep, back, full_gain)


def shards(query_rows, key_rows, value_rows, gain):
    seq_count, row_count, feat_count = query_rows.shape
    pair = [(0, 1), (1, 0)] if lax.axis_size("dp") == 2 else None
    if pair is None:
        full_gain = lax.all_gather(gain, "dp", axis=0, tiled=True).reshape(1, feat_count)
    else:
        other_gain = lax.ppermute(gain, "dp", pair)
        low_first = lax.axis_index("dp") == 0
        full_gain = jnp.concatenate([jnp.where(low_first, gain, other_gain),
                                     jnp.where(low_first, other_gain, gain)]).reshape(1, feat_count)
    query = query_rows.reshape(seq_count * row_count, feat_count)
    keyset = key_rows.reshape(seq_count * row_count, feat_count)
    valset = value_rows.reshape(seq_count * row_count, feat_count)
    state_terms = state_terms_of(keyset, valset, 16)
    keep, back = pair_chain_prefix(state_terms, "ctx", (8, 4, 2, 2))
    normed = attend_of(query, keyset, valset, keep, back, lax.axis_index("ctx") % 2, full_gain, 8)
    return normed.reshape(seq_count, row_count, feat_count)


def solution(mesh):
    in_specs = (
        P(("groups", "dp"), "ctx", None),
        P(("groups", "dp"), "ctx", None),
        P(("groups", "dp"), "ctx", None),
        P("dp"),
    )
    out_specs = P(("groups", "dp"), "ctx", None)
    return jax.shard_map(shards, mesh=mesh, in_specs=in_specs, out_specs=out_specs, check_vma=False)
```

```python
import jax
import jax.numpy as jnp
from jax import lax
from jax.experimental import pallas as pl
from jax.experimental.pallas import tpu as pltpu
from jax.sharding import PartitionSpec as P

H = 32


def pair_chain_prefix(terms, axis, pieces):
    count = lax.axis_size(axis)
    mine_at = lax.axis_index(axis) % 2
    first = mine_at == 0
    half = terms.shape[0] // 2
    pairs = count // 2
    mine_all = lax.dynamic_slice_in_dim(terms, mine_at * half, half, 0)
    other_all = lax.dynamic_slice_in_dim(terms, (1 - mine_at) * half, half, 0)
    swap = [(2 * i, 2 * i + 1) for i in range(pairs)] + [(2 * i + 1, 2 * i) for i in range(pairs)]
    step = half // pieces
    keeps, backs = [], []
    for piece in range(pieces):
        mine = mine_all[piece * step:(piece + 1) * step]
        got = lax.ppermute(other_all[piece * step:(piece + 1) * step], axis, swap)
        total = mine + got
        carried = jnp.zeros_like(total)
        for hop in range(1, pairs):
            links = [(2 * (hop - 1) + side, 2 * hop + side) for side in range(2)]
            carried = carried + lax.ppermute(carried + total, axis, links)
        keeps.append((carried + jnp.where(first, 0.0, got)).astype(jnp.bfloat16))
        send = (carried + jnp.where(first, mine, 0.0)).astype(jnp.bfloat16)
        backs.append(lax.ppermute(send, axis, swap))
    return jnp.concatenate(keeps, axis=0), jnp.concatenate(backs, axis=0)


def state_kernel(key_ref, val_ref, out_ref):
    heads, head_size, _ = out_ref.shape
    for head in range(heads):
        cols = slice(head * head_size, (head + 1) * head_size)
        out_ref[head] = lax.dot_general(
            key_ref[:, cols], val_ref[:, cols], (((0,), (0,)), ((), ())),
            preferred_element_type=jnp.float32)


def state_terms_of(keyset, valset, group):
    row_count, feat_count = keyset.shape
    head_size = feat_count // H
    width = group * head_size
    return pl.pallas_call(
        state_kernel,
        grid=(H // group,),
        in_specs=[pl.BlockSpec((row_count, width), lambda g: (0, g)),
                  pl.BlockSpec((row_count, width), lambda g: (0, g))],
        out_specs=pl.BlockSpec((group, head_size, head_size), lambda g: (g, 0, 0)),
        out_shape=jax.ShapeDtypeStruct((H, head_size, head_size), jnp.float32),
    )(keyset, valset)


def attend_heads(query_ref, key_ref, val_ref, prefix_ref, store, sumsq):
    row_count = query_ref.shape[0]
    heads, head_size, _ = prefix_ref.shape
    causal = (lax.broadcasted_iota(jnp.int32, (row_count, row_count), 0)
              >= lax.broadcasted_iota(jnp.int32, (row_count, row_count), 1))
    for head in range(heads):
        cols = slice(head * head_size, (head + 1) * head_size)
        query = query_ref[:, cols]
        scores = lax.dot_general(query, key_ref[:, cols], (((1,), (1,)), ((), ())),
                                 preferred_element_type=jnp.float32)
        weights = jnp.where(causal, scores, 0.0).astype(jnp.bfloat16)
        lhs = jnp.concatenate([weights, query], axis=1)
        rhs = jnp.concatenate([val_ref[:, cols], prefix_ref[head]], axis=0)
        attended = jnp.dot(lhs, rhs, preferred_element_type=jnp.float32)
        store(cols, attended)
        sumsq = sumsq + attended * attended
    return sumsq


def own_kernel(mine_ref, query_ref, key_ref, val_ref, keep_ref, att_ref, sumsq_ref):
    @pl.when(pl.program_id(0) == 0)
    def _():
        sumsq_ref[...] = jnp.zeros_like(sumsq_ref)

    def store(cols, attended):
        att_ref[:, cols] = attended

    sumsq_ref[...] = attend_heads(query_ref, key_ref, val_ref, keep_ref, store, sumsq_ref[...])


def other_kernel(mine_ref, query_ref, key_ref, val_ref, back_ref, own_ref, own_sumsq_ref, gain_ref, out_ref,
                 acc_ref, sumsq_ref):
    step = pl.program_id(0)
    row_count, width = query_ref.shape

    @pl.when(step == 0)
    def _():
        sumsq_ref[...] = own_sumsq_ref[...]

    def store(cols, attended):
        acc_ref[step, :, cols] = attended

    sumsq = attend_heads(query_ref, key_ref, val_ref, back_ref, store, sumsq_ref[...])
    sumsq_ref[...] = sumsq

    @pl.when(step == pl.num_programs(0) - 1)
    def _():
        total = jnp.sum(sumsq, axis=1, keepdims=True)
        feat_count = out_ref.shape[1]
        scale = lax.rsqrt(total / feat_count + 1e-05)
        half = feat_count // 2
        for own_at in range(2):
            @pl.when(mine_ref[0] == own_at)
            def _():
                own = slice(own_at * half, (own_at + 1) * half)
                out_ref[:, own] = (own_ref[...] * scale * gain_ref[:, own]).astype(out_ref.dtype)
                for part in range(acc_ref.shape[0]):
                    at = (1 - own_at) * half + part * width
                    cols = slice(at, at + width)
                    out_ref[:, cols] = (acc_ref[part] * scale * gain_ref[:, cols]).astype(out_ref.dtype)


def attend_of(query, keyset, valset, keep, back, mine_at, full_gain, group):
    row_count, feat_count = query.shape
    head_size = feat_count // H
    width = group * head_size
    steps = H // group // 2
    mine = jnp.reshape(mine_at, (1,)).astype(jnp.int32)
    own_spec = pl.BlockSpec((row_count, width), lambda g, at: (0, at[0] * steps + g))
    other_spec = pl.BlockSpec((row_count, width), lambda g, at: (0, (1 - at[0]) * steps + g))
    half_spec = pl.BlockSpec((group, head_size, head_size), lambda g, at: (g, 0, 0))
    sumsq_spec = pl.BlockSpec((row_count, head_size), lambda g, at: (0, 0))
    own, own_sumsq = pl.pallas_call(
        own_kernel,
        grid_spec=pltpu.PrefetchScalarGridSpec(
            num_scalar_prefetch=1,
            grid=(steps,),
            in_specs=[own_spec, own_spec, own_spec, half_spec],
            out_specs=[pl.BlockSpec((row_count, width), lambda g, at: (0, g)), sumsq_spec]),
        out_shape=[jax.ShapeDtypeStruct((row_count, feat_count // 2), jnp.float32),
                   jax.ShapeDtypeStruct((row_count, head_size), jnp.float32)],
    )(mine, query, keyset, valset, keep)
    return pl.pallas_call(
        other_kernel,
        grid_spec=pltpu.PrefetchScalarGridSpec(
            num_scalar_prefetch=1,
            grid=(steps,),
            in_specs=[other_spec, other_spec, other_spec, half_spec,
                      pl.BlockSpec((row_count, feat_count // 2), lambda g, at: (0, 0)),
                      sumsq_spec,
                      pl.BlockSpec((1, feat_count), lambda g, at: (0, 0))],
            out_specs=pl.BlockSpec((row_count, feat_count), lambda g, at: (0, 0)),
            scratch_shapes=[pltpu.VMEM((steps, row_count, width), jnp.float32),
                            pltpu.VMEM((row_count, head_size), jnp.float32)]),
        out_shape=jax.ShapeDtypeStruct((row_count, feat_count), jnp.bfloat16),
    )(mine, query, keyset, valset, back, own, own_sumsq, full_gain)


def shards(query_rows, key_rows, value_rows, gain):
    seq_count, row_count, feat_count = query_rows.shape
    pair = [(0, 1), (1, 0)] if lax.axis_size("dp") == 2 else None
    if pair is None:
        full_gain = lax.all_gather(gain, "dp", axis=0, tiled=True).reshape(1, feat_count)
    else:
        other_gain = lax.ppermute(gain, "dp", pair)
        low_first = lax.axis_index("dp") == 0
        full_gain = jnp.concatenate([jnp.where(low_first, gain, other_gain),
                                     jnp.where(low_first, other_gain, gain)]).reshape(1, feat_count)
    query = query_rows.reshape(seq_count * row_count, feat_count)
    keyset = key_rows.reshape(seq_count * row_count, feat_count)
    valset = value_rows.reshape(seq_count * row_count, feat_count)
    state_terms = state_terms_of(keyset, valset, 16)
    keep, back = pair_chain_prefix(state_terms, "ctx", 4)
    normed = attend_of(query, keyset, valset, keep, back, lax.axis_index("ctx") % 2, full_gain, 8)
    return normed.reshape(seq_count, row_count, feat_count)


def solution(mesh):
    in_specs = (
        P(("groups", "dp"), "ctx", None),
        P(("groups", "dp"), "ctx", None),
        P(("groups", "dp"), "ctx", None),
        P("dp"),
    )
    out_specs = P(("groups", "dp"), "ctx", None)
    return jax.shard_map(shards, mesh=mesh, in_specs=in_specs, out_specs=out_specs, check_vma=False)
```

```python
import jax
import jax.numpy as jnp
from jax import lax
from jax.experimental import pallas as pl
from jax.experimental.pallas import tpu as pltpu
from jax.sharding import PartitionSpec as P

H = 32


def pair_chain_prefix(terms, axis, pieces):
    count = lax.axis_size(axis)
    mine_at = lax.axis_index(axis) % 2
    first = mine_at == 0
    half = terms.shape[0] // 2
    pairs = count // 2
    mine_all = lax.dynamic_slice_in_dim(terms, mine_at * half, half, 0)
    other_all = lax.dynamic_slice_in_dim(terms, (1 - mine_at) * half, half, 0)
    swap = [(2 * i, 2 * i + 1) for i in range(pairs)] + [(2 * i + 1, 2 * i) for i in range(pairs)]
    step = half // pieces
    keeps, backs = [], []
    for piece in range(pieces):
        mine = mine_all[piece * step:(piece + 1) * step]
        got = lax.ppermute(other_all[piece * step:(piece + 1) * step], axis, swap)
        total = mine + got
        carried = jnp.zeros_like(total)
        for hop in range(1, pairs):
            links = [(2 * (hop - 1) + side, 2 * hop + side) for side in range(2)]
            carried = carried + lax.ppermute(carried + total, axis, links)
        keeps.append((carried + jnp.where(first, 0.0, got)).astype(jnp.bfloat16))
        send = (carried + jnp.where(first, mine, 0.0)).astype(jnp.bfloat16)
        backs.append(lax.ppermute(send, axis, swap))
    return jnp.concatenate(keeps, axis=0), backs


def state_kernel(key_ref, val_ref, out_ref):
    heads, head_size, _ = out_ref.shape
    for head in range(heads):
        cols = slice(head * head_size, (head + 1) * head_size)
        out_ref[head] = lax.dot_general(
            key_ref[:, cols], val_ref[:, cols], (((0,), (0,)), ((), ())),
            preferred_element_type=jnp.float32)


def state_terms_of(keyset, valset, group):
    row_count, feat_count = keyset.shape
    head_size = feat_count // H
    width = group * head_size
    return pl.pallas_call(
        state_kernel,
        grid=(H // group,),
        in_specs=[pl.BlockSpec((row_count, width), lambda g: (0, g)),
                  pl.BlockSpec((row_count, width), lambda g: (0, g))],
        out_specs=pl.BlockSpec((group, head_size, head_size), lambda g: (g, 0, 0)),
        out_shape=jax.ShapeDtypeStruct((H, head_size, head_size), jnp.float32),
    )(keyset, valset)


def attend_heads(query_ref, key_ref, val_ref, prefix_of, heads, store, sumsq):
    row_count, width = query_ref.shape
    head_size = width // heads
    causal = (lax.broadcasted_iota(jnp.int32, (row_count, row_count), 0)
              >= lax.broadcasted_iota(jnp.int32, (row_count, row_count), 1))
    for head in range(heads):
        cols = slice(head * head_size, (head + 1) * head_size)
        query = query_ref[:, cols]
        scores = lax.dot_general(query, key_ref[:, cols], (((1,), (1,)), ((), ())),
                                 preferred_element_type=jnp.float32)
        weights = jnp.where(causal, scores, 0.0).astype(jnp.bfloat16)
        lhs = jnp.concatenate([weights, query], axis=1)
        rhs = jnp.concatenate([val_ref[:, cols], prefix_of(head)], axis=0)
        attended = jnp.dot(lhs, rhs, preferred_element_type=jnp.float32)
        store(cols, attended)
        sumsq = sumsq + attended * attended
    return sumsq


def own_kernel(mine_ref, query_ref, key_ref, val_ref, keep_ref, att_ref, sumsq_ref):
    @pl.when(pl.program_id(0) == 0)
    def _():
        sumsq_ref[...] = jnp.zeros_like(sumsq_ref)

    def store(cols, attended):
        att_ref[:, cols] = attended

    sumsq_ref[...] = attend_heads(query_ref, key_ref, val_ref, lambda head: keep_ref[head],
                                  keep_ref.shape[0], store, sumsq_ref[...])


def other_kernel(mine_ref, query_ref, key_ref, val_ref, *refs):
    back_refs = refs[:-6]
    own_ref, own_sumsq_ref, gain_ref, out_ref, acc_ref, sumsq_ref = refs[-6:]
    step = pl.program_id(0)
    row_count, width = query_ref.shape
    per_piece = back_refs[0].shape[0]
    heads = width // (out_ref.shape[1] // H)
    per_step = heads // per_piece

    def prefix_of(head):
        pick = back_refs[head // per_piece][head % per_piece]
        for g in range(1, pl.num_programs(0)):
            pick = jnp.where(step == g, back_refs[g * per_step + head // per_piece][head % per_piece], pick)
        return pick

    @pl.when(step == 0)
    def _():
        sumsq_ref[...] = own_sumsq_ref[...]

    def store(cols, attended):
        acc_ref[step, :, cols] = attended

    sumsq = attend_heads(query_ref, key_ref, val_ref, prefix_of, heads, store, sumsq_ref[...])
    sumsq_ref[...] = sumsq

    @pl.when(step == pl.num_programs(0) - 1)
    def _():
        total = jnp.sum(sumsq, axis=1, keepdims=True)
        feat_count = out_ref.shape[1]
        scale = lax.rsqrt(total / feat_count + 1e-05)
        half = feat_count // 2
        for own_at in range(2):
            @pl.when(mine_ref[0] == own_at)
            def _():
                own = slice(own_at * half, (own_at + 1) * half)
                out_ref[:, own] = (own_ref[...] * scale * gain_ref[:, own]).astype(out_ref.dtype)
                for part in range(acc_ref.shape[0]):
                    at = (1 - own_at) * half + part * width
                    cols = slice(at, at + width)
                    out_ref[:, cols] = (acc_ref[part] * scale * gain_ref[:, cols]).astype(out_ref.dtype)


def attend_of(query, keyset, valset, keep, backs, mine_at, full_gain, group):
    row_count, feat_count = query.shape
    head_size = feat_count // H
    width = group * head_size
    steps = H // group // 2
    mine = jnp.reshape(mine_at, (1,)).astype(jnp.int32)
    own_spec = pl.BlockSpec((row_count, width), lambda g, at: (0, at[0] * steps + g))
    other_spec = pl.BlockSpec((row_count, width), lambda g, at: (0, (1 - at[0]) * steps + g))
    half_spec = pl.BlockSpec((group, head_size, head_size), lambda g, at: (g, 0, 0))
    sumsq_spec = pl.BlockSpec((row_count, head_size), lambda g, at: (0, 0))
    own, own_sumsq = pl.pallas_call(
        own_kernel,
        grid_spec=pltpu.PrefetchScalarGridSpec(
            num_scalar_prefetch=1,
            grid=(steps,),
            in_specs=[own_spec, own_spec, own_spec, half_spec],
            out_specs=[pl.BlockSpec((row_count, width), lambda g, at: (0, g)), sumsq_spec]),
        out_shape=[jax.ShapeDtypeStruct((row_count, feat_count // 2), jnp.float32),
                   jax.ShapeDtypeStruct((row_count, head_size), jnp.float32)],
    )(mine, query, keyset, valset, keep)
    return pl.pallas_call(
        other_kernel,
        grid_spec=pltpu.PrefetchScalarGridSpec(
            num_scalar_prefetch=1,
            grid=(steps,),
            in_specs=[other_spec, other_spec, other_spec]
                     + [pl.BlockSpec(piece.shape, lambda g, at: (0, 0, 0)) for piece in backs] + [
                      pl.BlockSpec((row_count, feat_count // 2), lambda g, at: (0, 0)),
                      sumsq_spec,
                      pl.BlockSpec((1, feat_count), lambda g, at: (0, 0))],
            out_specs=pl.BlockSpec((row_count, feat_count), lambda g, at: (0, 0)),
            scratch_shapes=[pltpu.VMEM((steps, row_count, width), jnp.float32),
                            pltpu.VMEM((row_count, head_size), jnp.float32)]),
        out_shape=jax.ShapeDtypeStruct((row_count, feat_count), jnp.bfloat16),
    )(mine, query, keyset, valset, *backs, own, own_sumsq, full_gain)


def shards(query_rows, key_rows, value_rows, gain):
    seq_count, row_count, feat_count = query_rows.shape
    pair = [(0, 1), (1, 0)] if lax.axis_size("dp") == 2 else None
    if pair is None:
        full_gain = lax.all_gather(gain, "dp", axis=0, tiled=True).reshape(1, feat_count)
    else:
        other_gain = lax.ppermute(gain, "dp", pair)
        low_first = lax.axis_index("dp") == 0
        full_gain = jnp.concatenate([jnp.where(low_first, gain, other_gain),
                                     jnp.where(low_first, other_gain, gain)]).reshape(1, feat_count)
    query = query_rows.reshape(seq_count * row_count, feat_count)
    keyset = key_rows.reshape(seq_count * row_count, feat_count)
    valset = value_rows.reshape(seq_count * row_count, feat_count)
    state_terms = state_terms_of(keyset, valset, 16)
    keep, backs = pair_chain_prefix(state_terms, "ctx", 4)
    normed = attend_of(query, keyset, valset, keep, backs, lax.axis_index("ctx") % 2, full_gain, 8)
    return normed.reshape(seq_count, row_count, feat_count)


def solution(mesh):
    in_specs = (
        P(("groups", "dp"), "ctx", None),
        P(("groups", "dp"), "ctx", None),
        P(("groups", "dp"), "ctx", None),
        P("dp"),
    )
    out_specs = P(("groups", "dp"), "ctx", None)
    return jax.shard_map(shards, mesh=mesh, in_specs=in_specs, out_specs=out_specs, check_vma=False)
```

```python
import jax
import jax.numpy as jnp
from jax import lax
from jax.experimental import pallas as pl
from jax.experimental.pallas import tpu as pltpu
from jax.sharding import PartitionSpec as P

H = 32


def pair_chain_prefix(terms, axis, pieces):
    count = lax.axis_size(axis)
    mine_at = lax.axis_index(axis) % 2
    first = mine_at == 0
    half = terms.shape[0] // 2
    pairs = count // 2
    mine_all = lax.dynamic_slice_in_dim(terms, mine_at * half, half, 0)
    other_all = lax.dynamic_slice_in_dim(terms, (1 - mine_at) * half, half, 0)
    swap = [(2 * i, 2 * i + 1) for i in range(pairs)] + [(2 * i + 1, 2 * i) for i in range(pairs)]
    step = half // pieces
    keeps, backs = [], []
    for piece in range(pieces):
        mine = mine_all[piece * step:(piece + 1) * step]
        got = lax.ppermute(other_all[piece * step:(piece + 1) * step], axis, swap)
        total = mine + got
        carried = jnp.zeros_like(total)
        for hop in range(1, pairs):
            links = [(2 * (hop - 1) + side, 2 * hop + side) for side in range(2)]
            carried = carried + lax.ppermute(carried + total, axis, links)
        keeps.append((carried + jnp.where(first, 0.0, got)).astype(jnp.bfloat16))
        send = (carried + jnp.where(first, mine, 0.0)).astype(jnp.bfloat16)
        backs.append(lax.ppermute(send, axis, swap))
    return jnp.concatenate(keeps, axis=0), backs


def state_kernel(key_ref, val_ref, out_ref):
    heads, head_size, _ = out_ref.shape
    for head in range(heads):
        cols = slice(head * head_size, (head + 1) * head_size)
        out_ref[head] = lax.dot_general(
            key_ref[:, cols], val_ref[:, cols], (((0,), (0,)), ((), ())),
            preferred_element_type=jnp.float32)


def state_terms_of(keyset, valset, group):
    row_count, feat_count = keyset.shape
    head_size = feat_count // H
    width = group * head_size
    return pl.pallas_call(
        state_kernel,
        grid=(H // group,),
        in_specs=[pl.BlockSpec((row_count, width), lambda g: (0, g)),
                  pl.BlockSpec((row_count, width), lambda g: (0, g))],
        out_specs=pl.BlockSpec((group, head_size, head_size), lambda g: (g, 0, 0)),
        out_shape=jax.ShapeDtypeStruct((H, head_size, head_size), jnp.float32),
    )(keyset, valset)


def attend_heads(query_ref, key_ref, val_ref, prefix_of, heads, store, sumsq):
    row_count, width = query_ref.shape
    head_size = width // heads
    causal = (lax.broadcasted_iota(jnp.int32, (row_count, row_count), 0)
              >= lax.broadcasted_iota(jnp.int32, (row_count, row_count), 1))
    for head in range(heads):
        cols = slice(head * head_size, (head + 1) * head_size)
        query = query_ref[:, cols]
        scores = lax.dot_general(query, key_ref[:, cols], (((1,), (1,)), ((), ())),
                                 preferred_element_type=jnp.float32)
        weights = jnp.where(causal, scores, 0.0).astype(jnp.bfloat16)
        lhs = jnp.concatenate([weights, query], axis=1)
        rhs = jnp.concatenate([val_ref[:, cols], prefix_of(head)], axis=0)
        attended = jnp.dot(lhs, rhs, preferred_element_type=jnp.float32)
        store(cols, attended)
        sumsq = sumsq + attended * attended
    return sumsq


def own_kernel(mine_ref, query_ref, key_ref, val_ref, keep_ref, att_ref, sumsq_ref):
    @pl.when(pl.program_id(0) == 0)
    def _():
        sumsq_ref[...] = jnp.zeros_like(sumsq_ref)

    def store(cols, attended):
        att_ref[:, cols] = attended

    sumsq_ref[...] = attend_heads(query_ref, key_ref, val_ref, lambda head: keep_ref[head],
                                  keep_ref.shape[0], store, sumsq_ref[...])


def other_kernel(mine_ref, query_ref, key_ref, val_ref, *refs):
    back_refs = refs[:-8]
    own_hbm, own_sumsq_ref, gain_ref, out_ref, acc_ref, sumsq_ref, own_ref, own_sem = refs[-8:]
    step = pl.program_id(0)
    own_copy = pltpu.make_async_copy(own_hbm, own_ref, own_sem)

    @pl.when(step == 0)
    def _():
        own_copy.start()
    row_count, width = query_ref.shape
    per_piece = back_refs[0].shape[0]
    heads = width // (out_ref.shape[1] // H)
    per_step = heads // per_piece

    def prefix_of(head):
        pick = back_refs[head // per_piece][head % per_piece]
        for g in range(1, pl.num_programs(0)):
            pick = jnp.where(step == g, back_refs[g * per_step + head // per_piece][head % per_piece], pick)
        return pick

    @pl.when(step == 0)
    def _():
        sumsq_ref[...] = own_sumsq_ref[...]

    def store(cols, attended):
        acc_ref[step, :, cols] = attended

    sumsq = attend_heads(query_ref, key_ref, val_ref, prefix_of, heads, store, sumsq_ref[...])
    sumsq_ref[...] = sumsq

    @pl.when(step == pl.num_programs(0) - 1)
    def _():
        total = jnp.sum(sumsq, axis=1, keepdims=True)
        feat_count = out_ref.shape[1]
        scale = lax.rsqrt(total / feat_count + 1e-05)
        half = feat_count // 2
        own_copy.wait()
        for own_at in range(2):
            @pl.when(mine_ref[0] == own_at)
            def _():
                own = slice(own_at * half, (own_at + 1) * half)
                out_ref[:, own] = (own_ref[...] * scale * gain_ref[:, own]).astype(out_ref.dtype)
                for part in range(acc_ref.shape[0]):
                    at = (1 - own_at) * half + part * width
                    cols = slice(at, at + width)
                    out_ref[:, cols] = (acc_ref[part] * scale * gain_ref[:, cols]).astype(out_ref.dtype)


def attend_of(query, keyset, valset, keep, backs, mine_at, full_gain, group):
    row_count, feat_count = query.shape
    head_size = feat_count // H
    width = group * head_size
    steps = H // group // 2
    mine = jnp.reshape(mine_at, (1,)).astype(jnp.int32)
    own_spec = pl.BlockSpec((row_count, width), lambda g, at: (0, at[0] * steps + g))
    other_spec = pl.BlockSpec((row_count, width), lambda g, at: (0, (1 - at[0]) * steps + g))
    half_spec = pl.BlockSpec((group, head_size, head_size), lambda g, at: (g, 0, 0))
    sumsq_spec = pl.BlockSpec((row_count, head_size), lambda g, at: (0, 0))
    own, own_sumsq = pl.pallas_call(
        own_kernel,
        grid_spec=pltpu.PrefetchScalarGridSpec(
            num_scalar_prefetch=1,
            grid=(steps,),
            in_specs=[own_spec, own_spec, own_spec, half_spec],
            out_specs=[pl.BlockSpec((row_count, width), lambda g, at: (0, g)), sumsq_spec]),
        out_shape=[jax.ShapeDtypeStruct((row_count, feat_count // 2), jnp.float32),
                   jax.ShapeDtypeStruct((row_count, head_size), jnp.float32)],
    )(mine, query, keyset, valset, keep)
    return pl.pallas_call(
        other_kernel,
        grid_spec=pltpu.PrefetchScalarGridSpec(
            num_scalar_prefetch=1,
            grid=(steps,),
            in_specs=[other_spec, other_spec, other_spec]
                     + [pl.BlockSpec(piece.shape, lambda g, at: (0, 0, 0)) for piece in backs] + [
                      pl.BlockSpec(memory_space=pl.ANY),
                      sumsq_spec,
                      pl.BlockSpec((1, feat_count), lambda g, at: (0, 0))],
            out_specs=pl.BlockSpec((row_count, feat_count), lambda g, at: (0, 0)),
            scratch_shapes=[pltpu.VMEM((steps, row_count, width), jnp.float32),
                            pltpu.VMEM((row_count, head_size), jnp.float32),
                            pltpu.VMEM((row_count, feat_count // 2), jnp.float32),
                            pltpu.SemaphoreType.DMA]),
        out_shape=jax.ShapeDtypeStruct((row_count, feat_count), jnp.bfloat16),
    )(mine, query, keyset, valset, *backs, own, own_sumsq, full_gain)


def shards(query_rows, key_rows, value_rows, gain):
    seq_count, row_count, feat_count = query_rows.shape
    pair = [(0, 1), (1, 0)] if lax.axis_size("dp") == 2 else None
    if pair is None:
        full_gain = lax.all_gather(gain, "dp", axis=0, tiled=True).reshape(1, feat_count)
    else:
        other_gain = lax.ppermute(gain, "dp", pair)
        low_first = lax.axis_index("dp") == 0
        full_gain = jnp.concatenate([jnp.where(low_first, gain, other_gain),
                                     jnp.where(low_first, other_gain, gain)]).reshape(1, feat_count)
    query = query_rows.reshape(seq_count * row_count, feat_count)
    keyset = key_rows.reshape(seq_count * row_count, feat_count)
    valset = value_rows.reshape(seq_count * row_count, feat_count)
    state_terms = state_terms_of(keyset, valset, 16)
    keep, backs = pair_chain_prefix(state_terms, "ctx", 4)
    normed = attend_of(query, keyset, valset, keep, backs, lax.axis_index("ctx") % 2, full_gain, 8)
    return normed.reshape(seq_count, row_count, feat_count)


def solution(mesh):
    in_specs = (
        P(("groups", "dp"), "ctx", None),
        P(("groups", "dp"), "ctx", None),
        P(("groups", "dp"), "ctx", None),
        P("dp"),
    )
    out_specs = P(("groups", "dp"), "ctx", None)
    return jax.shard_map(shards, mesh=mesh, in_specs=in_specs, out_specs=out_specs, check_vma=False)
```

```python
import jax
import jax.numpy as jnp
from jax import lax
from jax.experimental import pallas as pl
from jax.experimental.pallas import tpu as pltpu
from jax.sharding import PartitionSpec as P

H = 32


def pair_chain_prefix(terms, axis, pieces):
    count = lax.axis_size(axis)
    mine_at = lax.axis_index(axis) % 2
    first = mine_at == 0
    half = terms.shape[0] // 2
    pairs = count // 2
    mine_all = lax.dynamic_slice_in_dim(terms, mine_at * half, half, 0)
    other_all = lax.dynamic_slice_in_dim(terms, (1 - mine_at) * half, half, 0)
    swap = [(2 * i, 2 * i + 1) for i in range(pairs)] + [(2 * i + 1, 2 * i) for i in range(pairs)]
    step = half // pieces
    keeps, backs = [], []
    for piece in range(pieces):
        mine = mine_all[piece * step:(piece + 1) * step]
        got = lax.ppermute(other_all[piece * step:(piece + 1) * step], axis, swap)
        total = mine + got
        carried = jnp.zeros_like(total)
        for hop in range(1, pairs):
            links = [(2 * (hop - 1) + side, 2 * hop + side) for side in range(2)]
            carried = carried + lax.ppermute(carried + total, axis, links)
        keeps.append((carried + jnp.where(first, 0.0, got)).astype(jnp.bfloat16))
        send = (carried + jnp.where(first, mine, 0.0)).astype(jnp.bfloat16)
        backs.append(lax.ppermute(send, axis, swap))
    return keeps, backs


def state_kernel(key_ref, val_ref, out_ref):
    heads, head_size, _ = out_ref.shape
    for head in range(heads):
        cols = slice(head * head_size, (head + 1) * head_size)
        out_ref[head] = lax.dot_general(
            key_ref[:, cols], val_ref[:, cols], (((0,), (0,)), ((), ())),
            preferred_element_type=jnp.float32)


def state_terms_of(keyset, valset, group):
    row_count, feat_count = keyset.shape
    head_size = feat_count // H
    width = group * head_size
    return pl.pallas_call(
        state_kernel,
        grid=(H // group,),
        in_specs=[pl.BlockSpec((row_count, width), lambda g: (0, g)),
                  pl.BlockSpec((row_count, width), lambda g: (0, g))],
        out_specs=pl.BlockSpec((group, head_size, head_size), lambda g: (g, 0, 0)),
        out_shape=jax.ShapeDtypeStruct((H, head_size, head_size), jnp.float32),
    )(keyset, valset)


def attend_heads(query_ref, key_ref, val_ref, prefix_of, heads, store, sumsq):
    row_count, width = query_ref.shape
    head_size = width // heads
    causal = (lax.broadcasted_iota(jnp.int32, (row_count, row_count), 0)
              >= lax.broadcasted_iota(jnp.int32, (row_count, row_count), 1))
    for head in range(heads):
        cols = slice(head * head_size, (head + 1) * head_size)
        query = query_ref[:, cols]
        scores = lax.dot_general(query, key_ref[:, cols], (((1,), (1,)), ((), ())),
                                 preferred_element_type=jnp.float32)
        weights = jnp.where(causal, scores, 0.0).astype(jnp.bfloat16)
        lhs = jnp.concatenate([weights, query], axis=1)
        rhs = jnp.concatenate([val_ref[:, cols], prefix_of(head)], axis=0)
        attended = jnp.dot(lhs, rhs, preferred_element_type=jnp.float32)
        store(cols, attended)
        sumsq = sumsq + attended * attended
    return sumsq


def pick_piece(refs, heads):
    step = pl.program_id(0)
    per_piece = refs[0].shape[0]
    per_step = heads // per_piece

    def prefix_of(head):
        pick = refs[head // per_piece][head % per_piece]
        for g in range(1, pl.num_programs(0)):
            pick = jnp.where(step == g, refs[g * per_step + head // per_piece][head % per_piece], pick)
        return pick

    return prefix_of


def own_kernel(mine_ref, query_ref, key_ref, val_ref, *refs):
    keep_refs = refs[:-2]
    att_ref, sumsq_ref = refs[-2:]
    heads = att_ref.shape[1] // keep_refs[0].shape[1]

    @pl.when(pl.program_id(0) == 0)
    def _():
        sumsq_ref[...] = jnp.zeros_like(sumsq_ref)

    def store(cols, attended):
        att_ref[:, cols] = attended

    sumsq_ref[...] = attend_heads(query_ref, key_ref, val_ref, pick_piece(keep_refs, heads),
                                  heads, store, sumsq_ref[...])


def other_kernel(mine_ref, query_ref, key_ref, val_ref, *refs):
    back_refs = refs[:-8]
    own_hbm, own_sumsq_ref, gain_ref, out_ref, acc_ref, sumsq_ref, own_ref, own_sem = refs[-8:]
    step = pl.program_id(0)
    own_copy = pltpu.make_async_copy(own_hbm, own_ref, own_sem)

    @pl.when(step == 0)
    def _():
        own_copy.start()
    row_count, width = query_ref.shape
    heads = width // (out_ref.shape[1] // H)
    prefix_of = pick_piece(back_refs, heads)

    @pl.when(step == 0)
    def _():
        sumsq_ref[...] = own_sumsq_ref[...]

    def store(cols, attended):
        acc_ref[step, :, cols] = attended

    sumsq = attend_heads(query_ref, key_ref, val_ref, prefix_of, heads, store, sumsq_ref[...])
    sumsq_ref[...] = sumsq

    @pl.when(step == pl.num_programs(0) - 1)
    def _():
        total = jnp.sum(sumsq, axis=1, keepdims=True)
        feat_count = out_ref.shape[1]
        scale = lax.rsqrt(total / feat_count + 1e-05)
        half = feat_count // 2
        own_copy.wait()
        for own_at in range(2):
            @pl.when(mine_ref[0] == own_at)
            def _():
                own = slice(own_at * half, (own_at + 1) * half)
                out_ref[:, own] = (own_ref[...] * scale * gain_ref[:, own]).astype(out_ref.dtype)
                for part in range(acc_ref.shape[0]):
                    at = (1 - own_at) * half + part * width
                    cols = slice(at, at + width)
                    out_ref[:, cols] = (acc_ref[part] * scale * gain_ref[:, cols]).astype(out_ref.dtype)


def attend_of(query, keyset, valset, keeps, backs, mine_at, full_gain, group):
    row_count, feat_count = query.shape
    head_size = feat_count // H
    width = group * head_size
    steps = H // group // 2
    mine = jnp.reshape(mine_at, (1,)).astype(jnp.int32)
    own_spec = pl.BlockSpec((row_count, width), lambda g, at: (0, at[0] * steps + g))
    other_spec = pl.BlockSpec((row_count, width), lambda g, at: (0, (1 - at[0]) * steps + g))
    half_spec = pl.BlockSpec((group, head_size, head_size), lambda g, at: (g, 0, 0))
    sumsq_spec = pl.BlockSpec((row_count, head_size), lambda g, at: (0, 0))
    own, own_sumsq = pl.pallas_call(
        own_kernel,
        grid_spec=pltpu.PrefetchScalarGridSpec(
            num_scalar_prefetch=1,
            grid=(steps,),
            in_specs=[own_spec, own_spec, own_spec]
                     + [pl.BlockSpec(piece.shape, lambda g, at: (0, 0, 0)) for piece in keeps],
            out_specs=[pl.BlockSpec((row_count, width), lambda g, at: (0, g)), sumsq_spec]),
        out_shape=[jax.ShapeDtypeStruct((row_count, feat_count // 2), jnp.float32),
                   jax.ShapeDtypeStruct((row_count, head_size), jnp.float32)],
    )(mine, query, keyset, valset, *keeps)
    return pl.pallas_call(
        other_kernel,
        grid_spec=pltpu.PrefetchScalarGridSpec(
            num_scalar_prefetch=1,
            grid=(steps,),
            in_specs=[other_spec, other_spec, other_spec]
                     + [pl.BlockSpec(piece.shape, lambda g, at: (0, 0, 0)) for piece in backs] + [
                      pl.BlockSpec(memory_space=pl.ANY),
                      sumsq_spec,
                      pl.BlockSpec((1, feat_count), lambda g, at: (0, 0))],
            out_specs=pl.BlockSpec((row_count, feat_count), lambda g, at: (0, 0)),
            scratch_shapes=[pltpu.VMEM((steps, row_count, width), jnp.float32),
                            pltpu.VMEM((row_count, head_size), jnp.float32),
                            pltpu.VMEM((row_count, feat_count // 2), jnp.float32),
                            pltpu.SemaphoreType.DMA]),
        out_shape=jax.ShapeDtypeStruct((row_count, feat_count), jnp.bfloat16),
    )(mine, query, keyset, valset, *backs, own, own_sumsq, full_gain)


def shards(query_rows, key_rows, value_rows, gain):
    seq_count, row_count, feat_count = query_rows.shape
    pair = [(0, 1), (1, 0)] if lax.axis_size("dp") == 2 else None
    if pair is None:
        full_gain = lax.all_gather(gain, "dp", axis=0, tiled=True).reshape(1, feat_count)
    else:
        other_gain = lax.ppermute(gain, "dp", pair)
        low_first = lax.axis_index("dp") == 0
        full_gain = jnp.concatenate([jnp.where(low_first, gain, other_gain),
                                     jnp.where(low_first, other_gain, gain)]).reshape(1, feat_count)
    query = query_rows.reshape(seq_count * row_count, feat_count)
    keyset = key_rows.reshape(seq_count * row_count, feat_count)
    valset = value_rows.reshape(seq_count * row_count, feat_count)
    state_terms = state_terms_of(keyset, valset, 16)
    keeps, backs = pair_chain_prefix(state_terms, "ctx", 4)
    normed = attend_of(query, keyset, valset, keeps, backs, lax.axis_index("ctx") % 2, full_gain, 8)
    return normed.reshape(seq_count, row_count, feat_count)


def solution(mesh):
    in_specs = (
        P(("groups", "dp"), "ctx", None),
        P(("groups", "dp"), "ctx", None),
        P(("groups", "dp"), "ctx", None),
        P("dp"),
    )
    out_specs = P(("groups", "dp"), "ctx", None)
    return jax.shard_map(shards, mesh=mesh, in_specs=in_specs, out_specs=out_specs, check_vma=False)
```

```python
import jax
import jax.numpy as jnp
from jax import lax
from jax.experimental import pallas as pl
from jax.experimental.pallas import tpu as pltpu
from jax.sharding import PartitionSpec as P

H = 32


def pair_chain_prefix(terms, axis, pieces):
    count = lax.axis_size(axis)
    mine_at = lax.axis_index(axis) % 2
    first = mine_at == 0
    half = terms.shape[0] // 2
    pairs = count // 2
    mine_all = lax.dynamic_slice_in_dim(terms, mine_at * half, half, 0)
    other_all = lax.dynamic_slice_in_dim(terms, (1 - mine_at) * half, half, 0)
    swap = [(2 * i, 2 * i + 1) for i in range(pairs)] + [(2 * i + 1, 2 * i) for i in range(pairs)]
    step = half // pieces
    keeps, backs = [], []
    for piece in range(pieces):
        mine = mine_all[piece * step:(piece + 1) * step]
        got = lax.ppermute(other_all[piece * step:(piece + 1) * step], axis, swap)
        total = mine + got
        carried = jnp.zeros_like(total)
        for hop in range(1, pairs):
            links = [(2 * (hop - 1) + side, 2 * hop + side) for side in range(2)]
            carried = carried + lax.ppermute(carried + total, axis, links)
        keeps.append((carried, got))
        send = (carried + jnp.where(first, mine, 0.0)).astype(jnp.bfloat16)
        backs.append(lax.ppermute(send, axis, swap))
    return keeps, backs


def state_kernel(key_ref, val_ref, out_ref):
    heads, head_size, _ = out_ref.shape
    for head in range(heads):
        cols = slice(head * head_size, (head + 1) * head_size)
        out_ref[head] = lax.dot_general(
            key_ref[:, cols], val_ref[:, cols], (((0,), (0,)), ((), ())),
            preferred_element_type=jnp.float32)


def state_terms_of(keyset, valset, group):
    row_count, feat_count = keyset.shape
    head_size = feat_count // H
    width = group * head_size
    return pl.pallas_call(
        state_kernel,
        grid=(H // group,),
        in_specs=[pl.BlockSpec((row_count, width), lambda g: (0, g)),
                  pl.BlockSpec((row_count, width), lambda g: (0, g))],
        out_specs=pl.BlockSpec((group, head_size, head_size), lambda g: (g, 0, 0)),
        out_shape=jax.ShapeDtypeStruct((H, head_size, head_size), jnp.float32),
    )(keyset, valset)


def attend_heads(query_ref, key_ref, val_ref, prefix_of, heads, store, sumsq):
    row_count, width = query_ref.shape
    head_size = width // heads
    causal = (lax.broadcasted_iota(jnp.int32, (row_count, row_count), 0)
              >= lax.broadcasted_iota(jnp.int32, (row_count, row_count), 1))
    for head in range(heads):
        cols = slice(head * head_size, (head + 1) * head_size)
        query = query_ref[:, cols]
        scores = lax.dot_general(query, key_ref[:, cols], (((1,), (1,)), ((), ())),
                                 preferred_element_type=jnp.float32)
        weights = jnp.where(causal, scores, 0.0).astype(jnp.bfloat16)
        lhs = jnp.concatenate([weights, query], axis=1)
        rhs = jnp.concatenate([val_ref[:, cols], prefix_of(head)], axis=0)
        attended = jnp.dot(lhs, rhs, preferred_element_type=jnp.float32)
        store(cols, attended)
        sumsq = sumsq + attended * attended
    return sumsq


def pick_piece(refs, heads):
    step = pl.program_id(0)
    per_piece = refs[0].shape[0]
    per_step = heads // per_piece

    def prefix_of(head):
        pick = refs[head // per_piece][head % per_piece]
        for g in range(1, pl.num_programs(0)):
            pick = jnp.where(step == g, refs[g * per_step + head // per_piece][head % per_piece], pick)
        return pick

    return prefix_of


def own_kernel(mine_ref, query_ref, key_ref, val_ref, *refs):
    pieces = (len(refs) - 2) // 2
    carried_refs, got_refs = refs[:pieces], refs[pieces:2 * pieces]
    att_ref, sumsq_ref = refs[-2:]
    heads = att_ref.shape[1] // carried_refs[0].shape[1]
    carried_of = pick_piece(carried_refs, heads)
    got_of = pick_piece(got_refs, heads)
    second = mine_ref[0] == 1

    def keep_of(head):
        return (carried_of(head) + jnp.where(second, got_of(head), 0.0)).astype(jnp.bfloat16)

    @pl.when(pl.program_id(0) == 0)
    def _():
        sumsq_ref[...] = jnp.zeros_like(sumsq_ref)

    def store(cols, attended):
        att_ref[:, cols] = attended

    sumsq_ref[...] = attend_heads(query_ref, key_ref, val_ref, keep_of, heads, store, sumsq_ref[...])


def other_kernel(mine_ref, query_ref, key_ref, val_ref, *refs):
    back_refs = refs[:-8]
    own_hbm, own_sumsq_ref, gain_ref, out_ref, acc_ref, sumsq_ref, own_ref, own_sem = refs[-8:]
    step = pl.program_id(0)
    own_copy = pltpu.make_async_copy(own_hbm, own_ref, own_sem)

    @pl.when(step == 0)
    def _():
        own_copy.start()
    row_count, width = query_ref.shape
    heads = width // (out_ref.shape[1] // H)
    prefix_of = pick_piece(back_refs, heads)

    @pl.when(step == 0)
    def _():
        sumsq_ref[...] = own_sumsq_ref[...]

    def store(cols, attended):
        acc_ref[step, :, cols] = attended

    sumsq = attend_heads(query_ref, key_ref, val_ref, prefix_of, heads, store, sumsq_ref[...])
    sumsq_ref[...] = sumsq

    @pl.when(step == pl.num_programs(0) - 1)
    def _():
        total = jnp.sum(sumsq, axis=1, keepdims=True)
        feat_count = out_ref.shape[1]
        scale = lax.rsqrt(total / feat_count + 1e-05)
        half = feat_count // 2
        own_copy.wait()
        for own_at in range(2):
            @pl.when(mine_ref[0] == own_at)
            def _():
                own = slice(own_at * half, (own_at + 1) * half)
                out_ref[:, own] = (own_ref[...] * scale * gain_ref[:, own]).astype(out_ref.dtype)
                for part in range(acc_ref.shape[0]):
                    at = (1 - own_at) * half + part * width
                    cols = slice(at, at + width)
                    out_ref[:, cols] = (acc_ref[part] * scale * gain_ref[:, cols]).astype(out_ref.dtype)


def attend_of(query, keyset, valset, keeps, backs, mine_at, full_gain, group):
    row_count, feat_count = query.shape
    head_size = feat_count // H
    width = group * head_size
    steps = H // group // 2
    mine = jnp.reshape(mine_at, (1,)).astype(jnp.int32)
    own_spec = pl.BlockSpec((row_count, width), lambda g, at: (0, at[0] * steps + g))
    other_spec = pl.BlockSpec((row_count, width), lambda g, at: (0, (1 - at[0]) * steps + g))
    half_spec = pl.BlockSpec((group, head_size, head_size), lambda g, at: (g, 0, 0))
    sumsq_spec = pl.BlockSpec((row_count, head_size), lambda g, at: (0, 0))
    own, own_sumsq = pl.pallas_call(
        own_kernel,
        grid_spec=pltpu.PrefetchScalarGridSpec(
            num_scalar_prefetch=1,
            grid=(steps,),
            in_specs=[own_spec, own_spec, own_spec]
                     + [pl.BlockSpec(piece.shape, lambda g, at: (0, 0, 0)) for pair in keeps for piece in pair],
            out_specs=[pl.BlockSpec((row_count, width), lambda g, at: (0, g)), sumsq_spec]),
        out_shape=[jax.ShapeDtypeStruct((row_count, feat_count // 2), jnp.float32),
                   jax.ShapeDtypeStruct((row_count, head_size), jnp.float32)],
    )(mine, query, keyset, valset, *[pair[0] for pair in keeps], *[pair[1] for pair in keeps])
    return pl.pallas_call(
        other_kernel,
        grid_spec=pltpu.PrefetchScalarGridSpec(
            num_scalar_prefetch=1,
            grid=(steps,),
            in_specs=[other_spec, other_spec, other_spec]
                     + [pl.BlockSpec(piece.shape, lambda g, at: (0, 0, 0)) for piece in backs] + [
                      pl.BlockSpec(memory_space=pl.ANY),
                      sumsq_spec,
                      pl.BlockSpec((1, feat_count), lambda g, at: (0, 0))],
            out_specs=pl.BlockSpec((row_count, feat_count), lambda g, at: (0, 0)),
            scratch_shapes=[pltpu.VMEM((steps, row_count, width), jnp.float32),
                            pltpu.VMEM((row_count, head_size), jnp.float32),
                            pltpu.VMEM((row_count, feat_count // 2), jnp.float32),
                            pltpu.SemaphoreType.DMA]),
        out_shape=jax.ShapeDtypeStruct((row_count, feat_count), jnp.bfloat16),
    )(mine, query, keyset, valset, *backs, own, own_sumsq, full_gain)


def shards(query_rows, key_rows, value_rows, gain):
    seq_count, row_count, feat_count = query_rows.shape
    pair = [(0, 1), (1, 0)] if lax.axis_size("dp") == 2 else None
    if pair is None:
        full_gain = lax.all_gather(gain, "dp", axis=0, tiled=True).reshape(1, feat_count)
    else:
        other_gain = lax.ppermute(gain, "dp", pair)
        low_first = lax.axis_index("dp") == 0
        full_gain = jnp.concatenate([jnp.where(low_first, gain, other_gain),
                                     jnp.where(low_first, other_gain, gain)]).reshape(1, feat_count)
    query = query_rows.reshape(seq_count * row_count, feat_count)
    keyset = key_rows.reshape(seq_count * row_count, feat_count)
    valset = value_rows.reshape(seq_count * row_count, feat_count)
    state_terms = state_terms_of(keyset, valset, 16)
    keeps, backs = pair_chain_prefix(state_terms, "ctx", 4)
    normed = attend_of(query, keyset, valset, keeps, backs, lax.axis_index("ctx") % 2, full_gain, 8)
    return normed.reshape(seq_count, row_count, feat_count)


def solution(mesh):
    in_specs = (
        P(("groups", "dp"), "ctx", None),
        P(("groups", "dp"), "ctx", None),
        P(("groups", "dp"), "ctx", None),
        P("dp"),
    )
    out_specs = P(("groups", "dp"), "ctx", None)
    return jax.shard_map(shards, mesh=mesh, in_specs=in_specs, out_specs=out_specs, check_vma=False)
```

```python
import jax
import jax.numpy as jnp
from jax import lax
from jax.experimental import pallas as pl
from jax.experimental.pallas import tpu as pltpu
from jax.sharding import PartitionSpec as P

H = 32


def pair_chain_prefix(terms, axis, pieces):
    count = lax.axis_size(axis)
    mine_at = lax.axis_index(axis) % 2
    first = mine_at == 0
    half = terms.shape[0] // 2
    pairs = count // 2
    mine_all = lax.dynamic_slice_in_dim(terms, mine_at * half, half, 0)
    other_all = lax.dynamic_slice_in_dim(terms, (1 - mine_at) * half, half, 0)
    swap = [(2 * i, 2 * i + 1) for i in range(pairs)] + [(2 * i + 1, 2 * i) for i in range(pairs)]
    step = half // pieces
    keeps, backs = [], []
    for piece in range(pieces):
        mine = mine_all[piece * step:(piece + 1) * step]
        got = lax.ppermute(other_all[piece * step:(piece + 1) * step], axis, swap)
        total = mine + got
        carried = jnp.zeros_like(total)
        for hop in range(1, pairs):
            links = [(2 * (hop - 1) + side, 2 * hop + side) for side in range(2)]
            carried = carried + lax.ppermute(carried + total, axis, links)
        keeps.append((carried + jnp.where(first, 0.0, got)).astype(jnp.bfloat16))
        backs.append((carried + jnp.where(first, mine, 0.0)).astype(jnp.bfloat16))
    joined = [jnp.concatenate(backs[at:at + 2], axis=0) for at in range(0, len(backs), 2)]
    return keeps, [lax.ppermute(send, axis, swap) for send in joined]


def state_kernel(key_ref, val_ref, out_ref):
    heads, head_size, _ = out_ref.shape
    for head in range(heads):
        cols = slice(head * head_size, (head + 1) * head_size)
        out_ref[head] = lax.dot_general(
            key_ref[:, cols], val_ref[:, cols], (((0,), (0,)), ((), ())),
            preferred_element_type=jnp.float32)


def state_terms_of(keyset, valset, group):
    row_count, feat_count = keyset.shape
    head_size = feat_count // H
    width = group * head_size
    return pl.pallas_call(
        state_kernel,
        grid=(H // group,),
        in_specs=[pl.BlockSpec((row_count, width), lambda g: (0, g)),
                  pl.BlockSpec((row_count, width), lambda g: (0, g))],
        out_specs=pl.BlockSpec((group, head_size, head_size), lambda g: (g, 0, 0)),
        out_shape=jax.ShapeDtypeStruct((H, head_size, head_size), jnp.float32),
    )(keyset, valset)


def attend_heads(query_ref, key_ref, val_ref, prefix_of, heads, store, sumsq):
    row_count, width = query_ref.shape
    head_size = width // heads
    causal = (lax.broadcasted_iota(jnp.int32, (row_count, row_count), 0)
              >= lax.broadcasted_iota(jnp.int32, (row_count, row_count), 1))
    for head in range(heads):
        cols = slice(head * head_size, (head + 1) * head_size)
        query = query_ref[:, cols]
        scores = lax.dot_general(query, key_ref[:, cols], (((1,), (1,)), ((), ())),
                                 preferred_element_type=jnp.float32)
        weights = jnp.where(causal, scores, 0.0).astype(jnp.bfloat16)
        lhs = jnp.concatenate([weights, query], axis=1)
        rhs = jnp.concatenate([val_ref[:, cols], prefix_of(head)], axis=0)
        attended = jnp.dot(lhs, rhs, preferred_element_type=jnp.float32)
        store(cols, attended)
        sumsq = sumsq + attended * attended
    return sumsq


def pick_piece(refs, heads):
    step = pl.program_id(0)
    per_piece = refs[0].shape[0]
    per_step = heads // per_piece

    def prefix_of(head):
        pick = refs[head // per_piece][head % per_piece]
        for g in range(1, pl.num_programs(0)):
            pick = jnp.where(step == g, refs[g * per_step + head // per_piece][head % per_piece], pick)
        return pick

    return prefix_of


def own_kernel(mine_ref, query_ref, key_ref, val_ref, *refs):
    keep_refs = refs[:-2]
    att_ref, sumsq_ref = refs[-2:]
    heads = att_ref.shape[1] // keep_refs[0].shape[1]

    @pl.when(pl.program_id(0) == 0)
    def _():
        sumsq_ref[...] = jnp.zeros_like(sumsq_ref)

    def store(cols, attended):
        att_ref[:, cols] = attended

    sumsq_ref[...] = attend_heads(query_ref, key_ref, val_ref, pick_piece(keep_refs, heads),
                                  heads, store, sumsq_ref[...])


def other_kernel(mine_ref, query_ref, key_ref, val_ref, *refs):
    back_refs = refs[:-8]
    own_hbm, own_sumsq_ref, gain_ref, out_ref, acc_ref, sumsq_ref, own_ref, own_sem = refs[-8:]
    step = pl.program_id(0)
    own_copy = pltpu.make_async_copy(own_hbm, own_ref, own_sem)

    @pl.when(step == 0)
    def _():
        own_copy.start()
    row_count, width = query_ref.shape
    heads = width // (out_ref.shape[1] // H)
    prefix_of = pick_piece(back_refs, heads)

    @pl.when(step == 0)
    def _():
        sumsq_ref[...] = own_sumsq_ref[...]

    def store(cols, attended):
        acc_ref[step, :, cols] = attended

    sumsq = attend_heads(query_ref, key_ref, val_ref, prefix_of, heads, store, sumsq_ref[...])
    sumsq_ref[...] = sumsq

    @pl.when(step == pl.num_programs(0) - 1)
    def _():
        total = jnp.sum(sumsq, axis=1, keepdims=True)
        feat_count = out_ref.shape[1]
        scale = lax.rsqrt(total / feat_count + 1e-05)
        half = feat_count // 2
        own_copy.wait()
        for own_at in range(2):
            @pl.when(mine_ref[0] == own_at)
            def _():
                own = slice(own_at * half, (own_at + 1) * half)
                out_ref[:, own] = (own_ref[...] * scale * gain_ref[:, own]).astype(out_ref.dtype)
                for part in range(acc_ref.shape[0]):
                    at = (1 - own_at) * half + part * width
                    cols = slice(at, at + width)
                    out_ref[:, cols] = (acc_ref[part] * scale * gain_ref[:, cols]).astype(out_ref.dtype)


def attend_of(query, keyset, valset, keeps, backs, mine_at, full_gain, group):
    row_count, feat_count = query.shape
    head_size = feat_count // H
    width = group * head_size
    steps = H // group // 2
    mine = jnp.reshape(mine_at, (1,)).astype(jnp.int32)
    own_spec = pl.BlockSpec((row_count, width), lambda g, at: (0, at[0] * steps + g))
    other_spec = pl.BlockSpec((row_count, width), lambda g, at: (0, (1 - at[0]) * steps + g))
    half_spec = pl.BlockSpec((group, head_size, head_size), lambda g, at: (g, 0, 0))
    sumsq_spec = pl.BlockSpec((row_count, head_size), lambda g, at: (0, 0))
    own, own_sumsq = pl.pallas_call(
        own_kernel,
        grid_spec=pltpu.PrefetchScalarGridSpec(
            num_scalar_prefetch=1,
            grid=(steps,),
            in_specs=[own_spec, own_spec, own_spec]
                     + [pl.BlockSpec(piece.shape, lambda g, at: (0, 0, 0)) for piece in keeps],
            out_specs=[pl.BlockSpec((row_count, width), lambda g, at: (0, g)), sumsq_spec]),
        out_shape=[jax.ShapeDtypeStruct((row_count, feat_count // 2), jnp.float32),
                   jax.ShapeDtypeStruct((row_count, head_size), jnp.float32)],
    )(mine, query, keyset, valset, *keeps)
    return pl.pallas_call(
        other_kernel,
        grid_spec=pltpu.PrefetchScalarGridSpec(
            num_scalar_prefetch=1,
            grid=(steps,),
            in_specs=[other_spec, other_spec, other_spec]
                     + [pl.BlockSpec(piece.shape, lambda g, at: (0, 0, 0)) for piece in backs] + [
                      pl.BlockSpec(memory_space=pl.ANY),
                      sumsq_spec,
                      pl.BlockSpec((1, feat_count), lambda g, at: (0, 0))],
            out_specs=pl.BlockSpec((row_count, feat_count), lambda g, at: (0, 0)),
            scratch_shapes=[pltpu.VMEM((steps, row_count, width), jnp.float32),
                            pltpu.VMEM((row_count, head_size), jnp.float32),
                            pltpu.VMEM((row_count, feat_count // 2), jnp.float32),
                            pltpu.SemaphoreType.DMA]),
        out_shape=jax.ShapeDtypeStruct((row_count, feat_count), jnp.bfloat16),
    )(mine, query, keyset, valset, *backs, own, own_sumsq, full_gain)


def shards(query_rows, key_rows, value_rows, gain):
    seq_count, row_count, feat_count = query_rows.shape
    pair = [(0, 1), (1, 0)] if lax.axis_size("dp") == 2 else None
    if pair is None:
        full_gain = lax.all_gather(gain, "dp", axis=0, tiled=True).reshape(1, feat_count)
    else:
        other_gain = lax.ppermute(gain, "dp", pair)
        low_first = lax.axis_index("dp") == 0
        full_gain = jnp.concatenate([jnp.where(low_first, gain, other_gain),
                                     jnp.where(low_first, other_gain, gain)]).reshape(1, feat_count)
    query = query_rows.reshape(seq_count * row_count, feat_count)
    keyset = key_rows.reshape(seq_count * row_count, feat_count)
    valset = value_rows.reshape(seq_count * row_count, feat_count)
    state_terms = state_terms_of(keyset, valset, 16)
    keeps, backs = pair_chain_prefix(state_terms, "ctx", 4)
    normed = attend_of(query, keyset, valset, keeps, backs, lax.axis_index("ctx") % 2, full_gain, 8)
    return normed.reshape(seq_count, row_count, feat_count)


def solution(mesh):
    in_specs = (
        P(("groups", "dp"), "ctx", None),
        P(("groups", "dp"), "ctx", None),
        P(("groups", "dp"), "ctx", None),
        P("dp"),
    )
    out_specs = P(("groups", "dp"), "ctx", None)
    return jax.shard_map(shards, mesh=mesh, in_specs=in_specs, out_specs=out_specs, check_vma=False)
```

```python
import jax
import jax.numpy as jnp
from jax import lax
from jax.experimental import pallas as pl
from jax.experimental.pallas import tpu as pltpu
from jax.sharding import PartitionSpec as P

H = 32


def pair_chain_prefix(terms, axis, pieces):
    count = lax.axis_size(axis)
    mine_at = lax.axis_index(axis) % 2
    first = mine_at == 0
    half = terms.shape[0] // 2
    pairs = count // 2
    mine_all = lax.dynamic_slice_in_dim(terms, mine_at * half, half, 0)
    other_all = lax.dynamic_slice_in_dim(terms, (1 - mine_at) * half, half, 0)
    swap = [(2 * i, 2 * i + 1) for i in range(pairs)] + [(2 * i + 1, 2 * i) for i in range(pairs)]
    step = half // pieces
    keeps, backs = [], []
    for piece in range(pieces):
        mine = mine_all[piece * step:(piece + 1) * step]
        got = lax.ppermute(other_all[piece * step:(piece + 1) * step], axis, swap)
        total = mine + got
        carried = jnp.zeros_like(total)
        for hop in range(1, pairs):
            links = [(2 * (hop - 1) + side, 2 * hop + side) for side in range(2)]
            carried = carried + lax.ppermute(carried + total, axis, links)
        keeps.append((carried + jnp.where(first, 0.0, got)).astype(jnp.bfloat16))
        backs.append((carried + jnp.where(first, mine, 0.0)).astype(jnp.bfloat16))
    joined = [jnp.concatenate(backs, axis=0)]
    return keeps, [lax.ppermute(send, axis, swap) for send in joined]


def state_kernel(key_ref, val_ref, out_ref):
    heads, head_size, _ = out_ref.shape
    for head in range(heads):
        cols = slice(head * head_size, (head + 1) * head_size)
        out_ref[head] = lax.dot_general(
            key_ref[:, cols], val_ref[:, cols], (((0,), (0,)), ((), ())),
            preferred_element_type=jnp.float32)


def state_terms_of(keyset, valset, group):
    row_count, feat_count = keyset.shape
    head_size = feat_count // H
    width = group * head_size
    return pl.pallas_call(
        state_kernel,
        grid=(H // group,),
        in_specs=[pl.BlockSpec((row_count, width), lambda g: (0, g)),
                  pl.BlockSpec((row_count, width), lambda g: (0, g))],
        out_specs=pl.BlockSpec((group, head_size, head_size), lambda g: (g, 0, 0)),
        out_shape=jax.ShapeDtypeStruct((H, head_size, head_size), jnp.float32),
    )(keyset, valset)


def attend_heads(query_ref, key_ref, val_ref, prefix_of, heads, store, sumsq):
    row_count, width = query_ref.shape
    head_size = width // heads
    causal = (lax.broadcasted_iota(jnp.int32, (row_count, row_count), 0)
              >= lax.broadcasted_iota(jnp.int32, (row_count, row_count), 1))
    for head in range(heads):
        cols = slice(head * head_size, (head + 1) * head_size)
        query = query_ref[:, cols]
        scores = lax.dot_general(query, key_ref[:, cols], (((1,), (1,)), ((), ())),
                                 preferred_element_type=jnp.float32)
        weights = jnp.where(causal, scores, 0.0).astype(jnp.bfloat16)
        lhs = jnp.concatenate([weights, query], axis=1)
        rhs = jnp.concatenate([val_ref[:, cols], prefix_of(head)], axis=0)
        attended = jnp.dot(lhs, rhs, preferred_element_type=jnp.float32)
        store(cols, attended)
        sumsq = sumsq + attended * attended
    return sumsq


def pick_piece(refs, heads):
    step = pl.program_id(0)
    per_piece = refs[0].shape[0]
    per_step = heads // per_piece

    def prefix_of(head):
        if len(refs) == 1:
            return refs[0][step * heads + head]
        pick = refs[head // per_piece][head % per_piece]
        for g in range(1, pl.num_programs(0)):
            pick = jnp.where(step == g, refs[g * per_step + head // per_piece][head % per_piece], pick)
        return pick

    return prefix_of


def own_kernel(mine_ref, query_ref, key_ref, val_ref, *refs):
    keep_refs = refs[:-2]
    att_ref, sumsq_ref = refs[-2:]
    heads = att_ref.shape[1] // keep_refs[0].shape[1]

    @pl.when(pl.program_id(0) == 0)
    def _():
        sumsq_ref[...] = jnp.zeros_like(sumsq_ref)

    def store(cols, attended):
        att_ref[:, cols] = attended

    sumsq_ref[...] = attend_heads(query_ref, key_ref, val_ref, pick_piece(keep_refs, heads),
                                  heads, store, sumsq_ref[...])


def other_kernel(mine_ref, query_ref, key_ref, val_ref, *refs):
    back_refs = refs[:-8]
    own_hbm, own_sumsq_ref, gain_ref, out_ref, acc_ref, sumsq_ref, own_ref, own_sem = refs[-8:]
    step = pl.program_id(0)
    own_copy = pltpu.make_async_copy(own_hbm, own_ref, own_sem)

    @pl.when(step == 0)
    def _():
        own_copy.start()
    row_count, width = query_ref.shape
    heads = width // (out_ref.shape[1] // H)
    prefix_of = pick_piece(back_refs, heads)

    @pl.when(step == 0)
    def _():
        sumsq_ref[...] = own_sumsq_ref[...]

    def store(cols, attended):
        acc_ref[step, :, cols] = attended

    sumsq = attend_heads(query_ref, key_ref, val_ref, prefix_of, heads, store, sumsq_ref[...])
    sumsq_ref[...] = sumsq

    @pl.when(step == pl.num_programs(0) - 1)
    def _():
        total = jnp.sum(sumsq, axis=1, keepdims=True)
        feat_count = out_ref.shape[1]
        scale = lax.rsqrt(total / feat_count + 1e-05)
        half = feat_count // 2
        own_copy.wait()
        for own_at in range(2):
            @pl.when(mine_ref[0] == own_at)
            def _():
                own = slice(own_at * half, (own_at + 1) * half)
                out_ref[:, own] = (own_ref[...] * scale * gain_ref[:, own]).astype(out_ref.dtype)
                for part in range(acc_ref.shape[0]):
                    at = (1 - own_at) * half + part * width
                    cols = slice(at, at + width)
                    out_ref[:, cols] = (acc_ref[part] * scale * gain_ref[:, cols]).astype(out_ref.dtype)


def attend_of(query, keyset, valset, keeps, backs, mine_at, full_gain, group):
    row_count, feat_count = query.shape
    head_size = feat_count // H
    width = group * head_size
    steps = H // group // 2
    mine = jnp.reshape(mine_at, (1,)).astype(jnp.int32)
    own_spec = pl.BlockSpec((row_count, width), lambda g, at: (0, at[0] * steps + g))
    other_spec = pl.BlockSpec((row_count, width), lambda g, at: (0, (1 - at[0]) * steps + g))
    half_spec = pl.BlockSpec((group, head_size, head_size), lambda g, at: (g, 0, 0))
    sumsq_spec = pl.BlockSpec((row_count, head_size), lambda g, at: (0, 0))
    own, own_sumsq = pl.pallas_call(
        own_kernel,
        grid_spec=pltpu.PrefetchScalarGridSpec(
            num_scalar_prefetch=1,
            grid=(steps,),
            in_specs=[own_spec, own_spec, own_spec]
                     + [pl.BlockSpec(piece.shape, lambda g, at: (0, 0, 0)) for piece in keeps],
            out_specs=[pl.BlockSpec((row_count, width), lambda g, at: (0, g)), sumsq_spec]),
        out_shape=[jax.ShapeDtypeStruct((row_count, feat_count // 2), jnp.float32),
                   jax.ShapeDtypeStruct((row_count, head_size), jnp.float32)],
    )(mine, query, keyset, valset, *keeps)
    return pl.pallas_call(
        other_kernel,
        grid_spec=pltpu.PrefetchScalarGridSpec(
            num_scalar_prefetch=1,
            grid=(steps,),
            in_specs=[other_spec, other_spec, other_spec]
                     + [pl.BlockSpec(piece.shape, lambda g, at: (0, 0, 0)) for piece in backs] + [
                      pl.BlockSpec(memory_space=pl.ANY),
                      sumsq_spec,
                      pl.BlockSpec((1, feat_count), lambda g, at: (0, 0))],
            out_specs=pl.BlockSpec((row_count, feat_count), lambda g, at: (0, 0)),
            scratch_shapes=[pltpu.VMEM((steps, row_count, width), jnp.float32),
                            pltpu.VMEM((row_count, head_size), jnp.float32),
                            pltpu.VMEM((row_count, feat_count // 2), jnp.float32),
                            pltpu.SemaphoreType.DMA]),
        out_shape=jax.ShapeDtypeStruct((row_count, feat_count), jnp.bfloat16),
    )(mine, query, keyset, valset, *backs, own, own_sumsq, full_gain)


def shards(query_rows, key_rows, value_rows, gain):
    seq_count, row_count, feat_count = query_rows.shape
    pair = [(0, 1), (1, 0)] if lax.axis_size("dp") == 2 else None
    if pair is None:
        full_gain = lax.all_gather(gain, "dp", axis=0, tiled=True).reshape(1, feat_count)
    else:
        other_gain = lax.ppermute(gain, "dp", pair)
        low_first = lax.axis_index("dp") == 0
        full_gain = jnp.concatenate([jnp.where(low_first, gain, other_gain),
                                     jnp.where(low_first, other_gain, gain)]).reshape(1, feat_count)
    query = query_rows.reshape(seq_count * row_count, feat_count)
    keyset = key_rows.reshape(seq_count * row_count, feat_count)
    valset = value_rows.reshape(seq_count * row_count, feat_count)
    state_terms = state_terms_of(keyset, valset, 16)
    keeps, backs = pair_chain_prefix(state_terms, "ctx", 4)
    normed = attend_of(query, keyset, valset, keeps, backs, lax.axis_index("ctx") % 2, full_gain, 8)
    return normed.reshape(seq_count, row_count, feat_count)


def solution(mesh):
    in_specs = (
        P(("groups", "dp"), "ctx", None),
        P(("groups", "dp"), "ctx", None),
        P(("groups", "dp"), "ctx", None),
        P("dp"),
    )
    out_specs = P(("groups", "dp"), "ctx", None)
    return jax.shard_map(shards, mesh=mesh, in_specs=in_specs, out_specs=out_specs, check_vma=False)
```
